32 devices in a mesh: dp: 8 (over z, y), tensor: 4 (over x, core).
Axes of the slice: x: 2, y: 2, z: 4, core: 2. Of those that a mesh axis runs over, the one named last changes fastest.
Arguments:
- hidden: bfloat16 [2048, 1024], P('dp'), may hold values from -6 to 6
- lengths: int32 [8, 16], P('dp'), may hold values from 1 to 64, 256 in all within a row
- w_qkv: bfloat16 [3, 1024, 1024], P(None, None, 'tensor')
- b_qkv: float32 [3, 1024], P(None, 'tensor'), may hold values from -3 to 3
- w_output: bfloat16 [1024, 1024], P('tensor'), may hold values from -0.1875 to 0.1875
- b_output: float32 [1024], replicated, may hold values from -3 to 3
- first_gain: float32 [1024], replicated, may hold values from 0.25 to 1.75
- first_shift: float32 [1024], replicated, may hold values from -3 to 3
- w_up: bfloat16 [1024, 4096], P(None, 'tensor'), may hold values from -0.1875 to 0.1875
- b_up: float32 [4096], P('tensor'), may hold values from -3 to 3
- w_down: bfloat16 [4096, 1024], P('tensor'), may hold values from -0.09375 to 0.09375
- b_down: float32 [1024], replicated, may hold values from -3 to 3
- second_gain: float32 [1024], replicated, may hold values from 0.25 to 1.75
- second_shift: float32 [1024], replicated, may hold values from -3 to 3
- index: bfloat16 [16384, 1024], P('dp', 'tensor'), may hold values from -6 to 6
- candidates: int32 [128, 64], replicated, may hold values from 0 to 16383, as said below
Outputs:
- states: bfloat16 [2048, 1024], P('dp')
- scores: float32 [128, 64], P('dp')
The draws below stay inside these ranges and needn't reach their ends.
Inputs may be any that keep to these rules, and one draw needn't show every extreme that they name: `candidates`: each index of dp holds exactly 1024 of the 8192 named rows, counted with repetition.
All inputs are finite; a program needn't handle non-finite values.
Results may differ from the reference program's by a relative error of at most 0.014.
Values may be sent and summed in bfloat16 or wider, within the bound.
No kernel may reach another device: no remote copies, remote signals or barrier semaphores. Data moves between devices by JAX's collectives and lax.ppermute only.
A program may use at most 64 MiB of HBM per device.

```python
import math
import jax
import jax.numpy as jnp
import numpy as np
from jax import lax

D = 1024
FF = 4096
HEAD = 64
HEADS = 16
TOK_DEV = 256
TEXTS_DEV = 16
LONGEST = 64
CAND = 64
ROWS_DEV = 2048
TOKENS = 2048
TEXTS = 128
INDEX = 16384
N_DP = 8


def draw_hidden(key, part):
    return jnp.clip(jax.random.normal(key, (TOKENS, D), jnp.float32), -6.0, 6.0).astype(jnp.bfloat16)


def draw_w_qkv(key, part):
    drawn = jnp.clip(jax.random.normal(key, (3, D, D), jnp.float32), -6.0, 6.0) * D ** (-0.5)
    return drawn.astype(jnp.bfloat16)


def draw_candidates(key, part):
    first, second = jax.random.split(key)
    total = TEXTS * CAND
    order = jax.random.permutation(first, total).astype(jnp.int32)
    owner = order // (TEXTS_DEV * CAND)
    local = jax.random.randint(second, (total,), 0, ROWS_DEV, dtype=jnp.int32)
    return (owner * ROWS_DEV + local).reshape(TEXTS, CAND).astype(jnp.int32)


def levels(rng, dims, shards, least, largest):
    factor_of, own = 1.0, jax.random.fold_in(rng, 6)
    for axis_at, parts in shards:
        steps = jnp.exp(jax.random.uniform(jax.random.fold_in(own, axis_at), (parts,), jnp.float32, least / len(shards), largest / len(shards)))
        factor_of = factor_of * jnp.repeat(steps, dims[axis_at] // parts).reshape([-1 if axis == axis_at else 1 for axis in range(len(dims))])
    return factor_of


def split_up(number_of, total, reach, lean):
    loads = [(1 << 20) // math.isqrt(rank ** lean) + 1 for rank in range(2, number_of + 1)]
    spare, holding = total - reach - (number_of - 1), [1] * (number_of - 1)
    while spare > 0:
        free = [i for i in range(number_of - 1) if holding[i] < reach]
        mass, left = sum([loads[i] for i in free]), spare
        for i in free:
            more = min(reach - holding[i], max(1, left * loads[i] // mass), spare)
            holding[i] = holding[i] + more
            spare = spare - more
    return np.array([reach] + holding)


def ragged(stream_key, number_of, total, most, skew):
    if number_of == 2:
        one = jax.random.randint(stream_key, (), max(1, total - most), min(most, total - 1) + 1)
        return jnp.stack([one, total - one])
    sizes = jnp.asarray(split_up(number_of, total, most, skew), jnp.int32)
    couples = (number_of - 1) // 2
    donor, receiver = sizes[1:1 + 2 * couples:2], sizes[2:2 + 2 * couples:2]
    room = jnp.minimum(donor - 1, most - receiver)
    shifted = jax.random.randint(jax.random.fold_in(stream_key, 1), (couples,), 0, 1 << 20) % (room + 1)
    sizes = sizes.at[1:1 + 2 * couples:2].set(donor - shifted).at[2:2 + 2 * couples:2].set(receiver + shifted)
    return sizes[jax.random.permutation(jax.random.fold_in(stream_key, 2), number_of)]


def scatter_about(key, dims, scale, bound, pieces=(), held_as=jnp.bfloat16):
    loudness = levels(key, dims, pieces, -0.22, 0.18) if pieces else 1.0
    drawn = jax.random.normal(key, dims, jnp.float32) * scale * loudness
    return jnp.minimum(jnp.maximum(drawn, -bound), bound).astype(held_as)


def setup_inputs(seed: int = 0) -> dict:
    key_of = jax.random.split(jax.random.key(seed), 17)
    hidden = draw_hidden(jax.random.fold_in(key_of[16], 71), 0)
    lengths = jax.vmap(lambda own: ragged(own, TEXTS_DEV, TOK_DEV, LONGEST, 2))(jax.random.split(key_of[1], N_DP)).reshape((N_DP, TEXTS_DEV)).astype(jnp.int32)
    w_qkv = draw_w_qkv(jax.random.fold_in(key_of[16], 71), 0)
    b_qkv = scatter_about(key_of[3], (3, D), 0.5, 3.0, ((1, 4),), jnp.float32)
    w_output = scatter_about(key_of[4], (D, D), D ** -0.5, 0.1875, ((0, 4),))
    b_output = scatter_about(key_of[5], (D,), 0.5, 3.0, (), jnp.float32)
    first_gain = jnp.clip(1.0 + 0.15 * jax.random.normal(key_of[6], (D,), jnp.float32), 0.25, 1.75)
    first_shift = scatter_about(key_of[7], (D,), 0.5, 3.0, (), jnp.float32)
    w_up = scatter_about(key_of[8], (D, FF), D ** -0.5, 0.1875, ((1, 4),))
    b_up = scatter_about(key_of[9], (FF,), 0.5, 3.0, ((0, 4),), jnp.float32)
    w_down = scatter_about(key_of[10], (FF, D), FF ** -0.5, 0.09375, ((0, 4),))
    b_down = scatter_about(key_of[11], (D,), 0.5, 3.0, (), jnp.float32)
    second_gain = jnp.clip(1.0 + 0.15 * jax.random.normal(key_of[12], (D,), jnp.float32), 0.25, 1.75)
    second_shift = scatter_about(key_of[13], (D,), 0.5, 3.0, (), jnp.float32)
    index = scatter_about(key_of[14], (INDEX, D), 1.0, 6.0, ((0, 8), (1, 4)))
    candidates = draw_candidates(jax.random.fold_in(key_of[16], 71), 0)
    return dict(hidden=hidden, lengths=lengths, w_qkv=w_qkv, b_qkv=b_qkv, w_output=w_output, b_output=b_output, first_gain=first_gain, first_shift=first_shift, w_up=w_up, b_up=b_up, w_down=w_down, b_down=b_down, second_gain=second_gain, second_shift=second_shift, index=index, candidates=candidates)


def layer_norm(values, gain, shift):
    centre = lax.optimization_barrier(jnp.mean(values, axis=-1, keepdims=True))
    centred = values - centre
    spread = lax.optimization_barrier(jnp.mean(centred * centred, axis=-1, keepdims=True))
    return centred * lax.rsqrt(spread + 1e-05) * gain + shift

def segment_of(pack_lengths, count):
    ends = jnp.cumsum(pack_lengths)
    position = jnp.arange(count, dtype=jnp.int32)
    return lax.optimization_barrier(jnp.sum((position[:, None] >= ends[None, :]).astype(jnp.int32), axis=1)).astype(jnp.int32)

def reference(hidden, lengths, w_qkv, b_qkv, w_output, b_output, first_gain, first_shift, w_up, b_up, w_down, b_down, second_gain, second_shift, index, candidates):
    projected = [jnp.dot(hidden, w_qkv[j], preferred_element_type=jnp.float32) + b_qkv[j] for j in range(3)]
    queries = (projected[0] * 0.125).astype(jnp.bfloat16).reshape(N_DP, TOK_DEV, HEADS, HEAD)
    keys = projected[1].astype(jnp.bfloat16).reshape(N_DP, TOK_DEV, HEADS, HEAD)
    values = projected[2].astype(jnp.bfloat16).reshape(N_DP, TOK_DEV, HEADS, HEAD)

    def attend(packed):
        query_pack, key_pack, value_pack, pack_lengths = packed
        segment = segment_of(pack_lengths, TOK_DEV)
        same = segment[:, None] == segment[None, :]
        logits = jnp.einsum('thd,shd->hts', query_pack.astype(jnp.float32), key_pack.astype(jnp.float32))
        logits = jnp.where(same[None], logits, -1e+30)
        top = lax.optimization_barrier(jnp.max(logits, axis=-1, keepdims=True))
        expo = jnp.exp(logits - top)
        weights = (expo / lax.optimization_barrier(jnp.sum(expo, axis=-1, keepdims=True))).astype(jnp.bfloat16)
        context = jnp.einsum('hts,shd->thd', weights.astype(jnp.float32), value_pack.astype(jnp.float32))
        return context.astype(jnp.bfloat16)
    context = lax.map(attend, (queries, keys, values, lengths)).reshape(TOKENS, D)
    summed = jnp.dot(context, w_output, preferred_element_type=jnp.float32) + b_output + hidden.astype(jnp.float32)
    attended = layer_norm(summed, first_gain, first_shift).astype(jnp.bfloat16)
    activated = jax.nn.gelu(jnp.dot(attended, w_up, preferred_element_type=jnp.float32) + b_up, approximate=False).astype(jnp.bfloat16)
    output = jnp.dot(activated, w_down, preferred_element_type=jnp.float32) + b_down + attended.astype(jnp.float32)
    states = layer_norm(output, second_gain, second_shift).astype(jnp.bfloat16)

    def pool(packed):
        pack_states, pack_lengths = packed
        segment = segment_of(pack_lengths, TOK_DEV)
        member = (segment[None, :] == jnp.arange(TEXTS_DEV, dtype=jnp.int32)[:, None]).astype(jnp.float32)
        totals = jnp.dot(member, pack_states.astype(jnp.float32))
        return totals / pack_lengths.astype(jnp.float32)[:, None]
    pooled = lax.map(pool, (states.reshape(N_DP, TOK_DEV, D), lengths)).reshape(TEXTS, D)
    unit = (pooled * lax.rsqrt(lax.optimization_barrier(jnp.sum(pooled * pooled, axis=-1, keepdims=True)) + 1e-06)).astype(jnp.bfloat16)
    block_rows = math.gcd(TEXTS, 128)

    def score(packed):
        unit_block, wanted = packed
        fetched = jnp.take(index, wanted, axis=0)
        return jnp.einsum('rf,rcf->rc', unit_block.astype(jnp.float32), fetched.astype(jnp.float32))
    scores = lax.map(score, (unit.reshape(TEXTS // block_rows, block_rows, D), candidates.reshape(TEXTS // block_rows, block_rows, CAND)))
    return (states, scores.reshape(TEXTS, CAND))
```

```python
import math

import jax
import jax.numpy as jnp
from jax import lax
from jax.sharding import PartitionSpec as P

HEAD = 64


def layer_norm(values, gain, shift):
    centre = jnp.mean(values, axis=-1, keepdims=True)
    centred = values - centre
    spread = jnp.mean(centred * centred, axis=-1, keepdims=True)
    return centred * lax.rsqrt(spread + 1e-05) * gain + shift


def segment_of(pack_lengths, count):
    ends = jnp.cumsum(pack_lengths)
    position = jnp.arange(count, dtype=jnp.int32)
    return jnp.sum((position[:, None] >= ends[None, :]).astype(jnp.int32), axis=1)


def is_power_of_two(n):
    return n >= 1 and (n & (n - 1)) == 0


def xor_pairs(n, k):
    return [(i, i ^ k) for i in range(n)]


def levels_of(n):
    return [1 << j for j in range(int(math.log2(n)))] if n > 1 else []


def reduce_scatter_xor(value, axis, n, levels):
    index = lax.axis_index(axis)
    acc = value
    block = 0
    count = 1
    for k in levels:
        half = acc.shape[0] // 2
        bit = (index // k) % 2
        mine = lax.dynamic_slice_in_dim(acc, bit * half, half, 0)
        theirs = lax.dynamic_slice_in_dim(acc, (1 - bit) * half, half, 0)
        wire = jnp.float32 if value.dtype == jnp.float32 else jnp.bfloat16
        got = lax.ppermute(theirs.astype(wire), axis, xor_pairs(n, k))
        acc = mine.astype(jnp.float32) + got.astype(jnp.float32)
        count *= 2
        block = block * 2 + bit
    return acc, block


def all_gather_xor(value, axis, n, levels):
    index = lax.axis_index(axis)
    cur = value
    for k in levels:
        other = lax.ppermute(cur, axis, xor_pairs(n, k))
        bit = (index // k) % 2
        cur = jnp.where(bit == 0, jnp.concatenate([cur, other]), jnp.concatenate([other, cur]))
    return cur


def settle(partial_value, residual, bias, gain, shift, n_tensor):
    if not is_power_of_two(n_tensor) or partial_value.shape[0] % n_tensor:
        total = lax.psum(partial_value.astype(jnp.bfloat16), "tensor").astype(jnp.float32)
        return layer_norm(total + bias + residual.astype(jnp.float32), gain, shift).astype(
            jnp.bfloat16
        )
    levels = levels_of(n_tensor)
    total, block = reduce_scatter_xor(partial_value.astype(jnp.bfloat16), "tensor", n_tensor, levels)
    rows = total.shape[0]
    own_residual = lax.dynamic_slice_in_dim(residual, block * rows, rows, 0)
    normed = layer_norm(total + bias + own_residual.astype(jnp.float32), gain, shift).astype(
        jnp.bfloat16
    )
    return all_gather_xor(normed, "tensor", n_tensor, levels[::-1])


def body(
    hidden,
    lengths,
    w_qkv,
    b_qkv,
    w_output,
    b_output,
    first_gain,
    first_shift,
    w_up,
    b_up,
    w_down,
    b_down,
    second_gain,
    second_shift,
    index,
    candidates,
    n_dp,
    n_tensor,
):
    tokens_here = hidden.shape[0]
    local_width = w_qkv.shape[2]
    local_heads = local_width // HEAD
    projected = [
        jnp.dot(hidden, w_qkv[j], preferred_element_type=jnp.float32) + b_qkv[j] for j in range(3)
    ]
    queries = (projected[0] * 0.125).astype(jnp.bfloat16).reshape(tokens_here, local_heads, HEAD)
    keys = projected[1].astype(jnp.bfloat16).reshape(tokens_here, local_heads, HEAD)
    values = projected[2].astype(jnp.bfloat16).reshape(tokens_here, local_heads, HEAD)
    segment = segment_of(lengths[0], tokens_here)
    same = segment[:, None] == segment[None, :]
    logits = jnp.einsum("thd,shd->hts", queries, keys, preferred_element_type=jnp.float32)
    logits = jnp.where(same[None], logits, -1e30)
    top = jnp.max(logits, axis=-1, keepdims=True)
    expo = jnp.exp(logits - top)
    weights = (expo / jnp.sum(expo, axis=-1, keepdims=True)).astype(jnp.bfloat16)
    context = jnp.einsum("hts,shd->thd", weights, values, preferred_element_type=jnp.float32)
    context = context.astype(jnp.bfloat16).reshape(tokens_here, local_width)
    partial_value = jnp.dot(context, w_output, preferred_element_type=jnp.float32)
    attended = settle(partial_value, hidden, b_output, first_gain, first_shift, n_tensor)
    activated = jax.nn.gelu(
        jnp.dot(attended, w_up, preferred_element_type=jnp.float32) + b_up, approximate=False
    ).astype(jnp.bfloat16)
    partial_value = jnp.dot(activated, w_down, preferred_element_type=jnp.float32)
    states = settle(partial_value, attended, b_down, second_gain, second_shift, n_tensor)
    texts_here = lengths.shape[1]
    member = (segment[None, :] == jnp.arange(texts_here, dtype=jnp.int32)[:, None]).astype(
        jnp.bfloat16
    )
    pooled = (
        jnp.dot(member, states, preferred_element_type=jnp.float32)
        / lengths[0].astype(jnp.float32)[:, None]
    )
    unit = pooled * lax.rsqrt(jnp.sum(pooled * pooled, axis=-1, keepdims=True) + 1e-06)
    quarter = index.shape[1]
    unit_quarter = lax.dynamic_slice_in_dim(
        unit, lax.axis_index("tensor") * quarter, quarter, 1
    ).astype(jnp.bfloat16)
    row_base = lax.axis_index("dp") * index.shape[0]
    xor_ok = (
        is_power_of_two(n_dp)
        and is_power_of_two(n_tensor)
        and candidates.shape[0] % n_dp == 0
    )
    if xor_ok:
        gathered = all_gather_xor(unit_quarter, "dp", n_dp, levels_of(n_dp))
    else:
        gathered = lax.all_gather(unit_quarter, "dp", axis=0, tiled=True)
    all_texts = candidates.shape[0]
    cand_count = candidates.shape[1]
    shard_rows = index.shape[0]
    block_rows = math.gcd(all_texts, 128)
    block_count = all_texts // block_rows
    local_rows = candidates - row_base
    row_ids = jnp.arange(shard_rows, dtype=jnp.int32)

    def score_block(packed):
        query_block, wanted = packed
        tile = lax.dot_general(
            query_block, index, (((1,), (1,)), ((), ())), preferred_element_type=jnp.float32
        )
        chosen = wanted[:, :, None] == row_ids[None, None, :]
        return jnp.sum(jnp.where(chosen, tile[:, None, :], 0.0), axis=2)

    partial_scores = lax.map(
        score_block,
        (
            gathered.reshape(block_count, block_rows, quarter),
            local_rows.reshape(block_count, block_rows, cand_count),
        ),
    )
    partial_scores = partial_scores.reshape(all_texts, cand_count)
    if not xor_ok:
        slice_scores = lax.psum_scatter(
            partial_scores, ("dp", "tensor"), scatter_dimension=0, tiled=True
        )
        scores = lax.all_gather(slice_scores, "tensor", axis=0, tiled=True)
        return (states, scores)
    text_scores, _ = reduce_scatter_xor(partial_scores, "dp", n_dp, levels_of(n_dp)[::-1])
    for k in levels_of(n_tensor):
        text_scores = text_scores + lax.ppermute(text_scores, "tensor", xor_pairs(n_tensor, k))
    return (states, text_scores)


def solution(mesh):
    placed = (
        P("dp", None),
        P("dp", None),
        P(None, None, "tensor"),
        P(None, "tensor"),
        P("tensor", None),
        P(),
        P(),
        P(),
        P(None, "tensor"),
        P("tensor"),
        P("tensor", None),
        P(),
        P(),
        P(),
        P("dp", "tensor"),
        P(),
    )
    n_dp = mesh.shape["dp"]
    n_tensor = mesh.shape["tensor"]

    def run(*args):
        return body(*args, n_dp=n_dp, n_tensor=n_tensor)

    return jax.shard_map(
        run, mesh=mesh, in_specs=placed, out_specs=(P("dp", None), P("dp", None)), check_vma=False
    )
```

```python
import math

import jax
import jax.numpy as jnp
from jax import lax
from jax.sharding import PartitionSpec as P

HEAD = 64


def layer_norm(values, gain, shift):
    centre = jnp.mean(values, axis=-1, keepdims=True)
    centred = values - centre
    spread = jnp.mean(centred * centred, axis=-1, keepdims=True)
    return centred * lax.rsqrt(spread + 1e-05) * gain + shift


def segment_of(pack_lengths, count):
    ends = jnp.cumsum(pack_lengths)
    position = jnp.arange(count, dtype=jnp.int32)
    return jnp.sum((position[:, None] >= ends[None, :]).astype(jnp.int32), axis=1)


def is_power_of_two(n):
    return n >= 1 and (n & (n - 1)) == 0


def xor_pairs(n, k):
    return [(i, i ^ k) for i in range(n)]


def levels_of(n):
    return [1 << j for j in range(int(math.log2(n)))] if n > 1 else []


def reduce_scatter_xor(value, axis, n, levels):
    index = lax.axis_index(axis)
    acc = value
    block = 0
    count = 1
    for k in levels:
        half = acc.shape[0] // 2
        bit = (index // k) % 2
        mine = lax.dynamic_slice_in_dim(acc, bit * half, half, 0)
        theirs = lax.dynamic_slice_in_dim(acc, (1 - bit) * half, half, 0)
        wire = jnp.float32 if value.dtype == jnp.float32 else jnp.bfloat16
        got = lax.ppermute(theirs.astype(wire), axis, xor_pairs(n, k))
        acc = mine.astype(jnp.float32) + got.astype(jnp.float32)
        count *= 2
        block = block * 2 + bit
    return acc, block


def all_gather_xor(value, axis, n, levels):
    index = lax.axis_index(axis)
    cur = value
    for k in levels:
        other = lax.ppermute(cur, axis, xor_pairs(n, k))
        bit = (index // k) % 2
        cur = jnp.where(bit == 0, jnp.concatenate([cur, other]), jnp.concatenate([other, cur]))
    return cur


def settle(partial_value, residual, bias, gain, shift, n_tensor):
    if not is_power_of_two(n_tensor) or partial_value.shape[0] % n_tensor:
        total = lax.psum(partial_value.astype(jnp.bfloat16), "tensor").astype(jnp.float32)
        return layer_norm(total + bias + residual.astype(jnp.float32), gain, shift).astype(
            jnp.bfloat16
        )
    levels = levels_of(n_tensor)
    total, block = reduce_scatter_xor(partial_value.astype(jnp.bfloat16), "tensor", n_tensor, levels)
    rows = total.shape[0]
    own_residual = lax.dynamic_slice_in_dim(residual, block * rows, rows, 0)
    normed = layer_norm(total + bias + own_residual.astype(jnp.float32), gain, shift).astype(
        jnp.bfloat16
    )
    return all_gather_xor(normed, "tensor", n_tensor, levels[::-1])


def body(
    hidden,
    lengths,
    w_qkv,
    b_qkv,
    w_output,
    b_output,
    first_gain,
    first_shift,
    w_up,
    b_up,
    w_down,
    b_down,
    second_gain,
    second_shift,
    index,
    candidates,
    n_dp,
    n_tensor,
):
    tokens_here = hidden.shape[0]
    local_width = w_qkv.shape[2]
    local_heads = local_width // HEAD
    projected = [
        jnp.dot(hidden, w_qkv[j], preferred_element_type=jnp.float32) + b_qkv[j] for j in range(3)
    ]
    queries = (projected[0] * 0.125).astype(jnp.bfloat16).reshape(tokens_here, local_heads, HEAD)
    keys = projected[1].astype(jnp.bfloat16).reshape(tokens_here, local_heads, HEAD)
    values = projected[2].astype(jnp.bfloat16).reshape(tokens_here, local_heads, HEAD)
    segment = segment_of(lengths[0], tokens_here)
    same = segment[:, None] == segment[None, :]
    logits = jnp.einsum("thd,shd->hts", queries, keys, preferred_element_type=jnp.float32)
    logits = jnp.where(same[None], logits, -1e30)
    top = jnp.max(logits, axis=-1, keepdims=True)
    expo = jnp.exp(logits - top)
    weights = (expo / jnp.sum(expo, axis=-1, keepdims=True)).astype(jnp.bfloat16)
    context = jnp.einsum("hts,shd->thd", weights, values, preferred_element_type=jnp.float32)
    context = context.astype(jnp.bfloat16).reshape(tokens_here, local_width)
    partial_value = jnp.dot(context, w_output, preferred_element_type=jnp.float32)
    attended = settle(partial_value, hidden, b_output, first_gain, first_shift, n_tensor)
    activated = jax.nn.gelu(
        jnp.dot(attended, w_up, preferred_element_type=jnp.float32) + b_up, approximate=False
    ).astype(jnp.bfloat16)
    partial_value = jnp.dot(activated, w_down, preferred_element_type=jnp.float32)
    states = settle(partial_value, attended, b_down, second_gain, second_shift, n_tensor)
    texts_here = lengths.shape[1]
    member = (segment[None, :] == jnp.arange(texts_here, dtype=jnp.int32)[:, None]).astype(
        jnp.bfloat16
    )
    pooled = (
        jnp.dot(member, states, preferred_element_type=jnp.float32)
        / lengths[0].astype(jnp.float32)[:, None]
    )
    unit = pooled * lax.rsqrt(jnp.sum(pooled * pooled, axis=-1, keepdims=True) + 1e-06)
    quarter = index.shape[1]
    unit_quarter = lax.dynamic_slice_in_dim(
        unit, lax.axis_index("tensor") * quarter, quarter, 1
    ).astype(jnp.bfloat16)
    row_base = lax.axis_index("dp") * index.shape[0]
    xor_ok = (
        is_power_of_two(n_dp)
        and is_power_of_two(n_tensor)
        and candidates.shape[0] % n_dp == 0
    )
    if xor_ok:
        gathered = all_gather_xor(unit_quarter, "dp", n_dp, levels_of(n_dp))
    else:
        gathered = lax.all_gather(unit_quarter, "dp", axis=0, tiled=True)
    all_texts = candidates.shape[0]
    shard_rows = index.shape[0]
    local_rows = candidates - row_base
    held = (local_rows >= 0) & (local_rows < shard_rows)
    tile = lax.dot_general(
        gathered, index, (((1,), (1,)), ((), ())), preferred_element_type=jnp.float32
    )
    picked = jnp.take_along_axis(tile, jnp.clip(local_rows, 0, shard_rows - 1), axis=1)
    partial_scores = jnp.where(held, picked, 0.0)
    if not xor_ok:
        slice_scores = lax.psum_scatter(
            partial_scores, ("dp", "tensor"), scatter_dimension=0, tiled=True
        )
        scores = lax.all_gather(slice_scores, "tensor", axis=0, tiled=True)
        return (states, scores)
    text_scores, _ = reduce_scatter_xor(partial_scores, "dp", n_dp, levels_of(n_dp)[::-1])
    for k in levels_of(n_tensor):
        text_scores = text_scores + lax.ppermute(text_scores, "tensor", xor_pairs(n_tensor, k))
    return (states, text_scores)


def solution(mesh):
    placed = (
        P("dp", None),
        P("dp", None),
        P(None, None, "tensor"),
        P(None, "tensor"),
        P("tensor", None),
        P(),
        P(),
        P(),
        P(None, "tensor"),
        P("tensor"),
        P("tensor", None),
        P(),
        P(),
        P(),
        P("dp", "tensor"),
        P(),
    )
    n_dp = mesh.shape["dp"]
    n_tensor = mesh.shape["tensor"]

    def run(*args):
        return body(*args, n_dp=n_dp, n_tensor=n_tensor)

    return jax.shard_map(
        run, mesh=mesh, in_specs=placed, out_specs=(P("dp", None), P("dp", None)), check_vma=False
    )
```

```python
import math

import jax
import jax.numpy as jnp
from jax import lax
from jax.sharding import PartitionSpec as P

HEAD = 64


def layer_norm(values, gain, shift):
    centre = jnp.mean(values, axis=-1, keepdims=True)
    centred = values - centre
    spread = jnp.mean(centred * centred, axis=-1, keepdims=True)
    return centred * lax.rsqrt(spread + 1e-05) * gain + shift


def segment_of(pack_lengths, count):
    ends = jnp.cumsum(pack_lengths)
    position = jnp.arange(count, dtype=jnp.int32)
    return jnp.sum((position[:, None] >= ends[None, :]).astype(jnp.int32), axis=1)


def is_power_of_two(n):
    return n >= 1 and (n & (n - 1)) == 0


def xor_pairs(n, k):
    return [(i, i ^ k) for i in range(n)]


def levels_of(n):
    return [1 << j for j in range(int(math.log2(n)))] if n > 1 else []


def reduce_scatter_xor(value, axis, n, levels):
    index = lax.axis_index(axis)
    acc = value
    block = 0
    count = 1
    for k in levels:
        half = acc.shape[0] // 2
        bit = (index // k) % 2
        mine = lax.dynamic_slice_in_dim(acc, bit * half, half, 0)
        theirs = lax.dynamic_slice_in_dim(acc, (1 - bit) * half, half, 0)
        wire = jnp.float32 if value.dtype == jnp.float32 else jnp.bfloat16
        got = lax.ppermute(theirs.astype(wire), axis, xor_pairs(n, k))
        acc = mine.astype(jnp.float32) + got.astype(jnp.float32)
        count *= 2
        block = block * 2 + bit
    return acc, block


def all_gather_xor(value, axis, n, levels):
    index = lax.axis_index(axis)
    cur = value
    for k in levels:
        other = lax.ppermute(cur, axis, xor_pairs(n, k))
        bit = (index // k) % 2
        cur = jnp.where(bit == 0, jnp.concatenate([cur, other]), jnp.concatenate([other, cur]))
    return cur


def settle(partial_value, residual, bias, gain, shift, n_tensor):
    if not is_power_of_two(n_tensor) or partial_value.shape[0] % n_tensor:
        total = lax.psum(partial_value.astype(jnp.bfloat16), "tensor").astype(jnp.float32)
        return layer_norm(total + bias + residual.astype(jnp.float32), gain, shift).astype(
            jnp.bfloat16
        )
    levels = levels_of(n_tensor)
    total, block = reduce_scatter_xor(partial_value.astype(jnp.bfloat16), "tensor", n_tensor, levels)
    rows = total.shape[0]
    own_residual = lax.dynamic_slice_in_dim(residual, block * rows, rows, 0)
    normed = layer_norm(total + bias + own_residual.astype(jnp.float32), gain, shift).astype(
        jnp.bfloat16
    )
    return all_gather_xor(normed, "tensor", n_tensor, levels[::-1])


def body(
    hidden,
    lengths,
    w_qkv,
    b_qkv,
    w_output,
    b_output,
    first_gain,
    first_shift,
    w_up,
    b_up,
    w_down,
    b_down,
    second_gain,
    second_shift,
    index,
    candidates,
    n_dp,
    n_tensor,
):
    tokens_here = hidden.shape[0]
    local_width = w_qkv.shape[2]
    local_heads = local_width // HEAD
    projected = [
        jnp.dot(hidden, w_qkv[j], preferred_element_type=jnp.float32) + b_qkv[j] for j in range(3)
    ]
    queries = (projected[0] * 0.125).astype(jnp.bfloat16).reshape(tokens_here, local_heads, HEAD)
    keys = projected[1].astype(jnp.bfloat16).reshape(tokens_here, local_heads, HEAD)
    values = projected[2].astype(jnp.bfloat16).reshape(tokens_here, local_heads, HEAD)
    segment = segment_of(lengths[0], tokens_here)
    same = segment[:, None] == segment[None, :]
    logits = jnp.einsum("thd,shd->hts", queries, keys, preferred_element_type=jnp.float32)
    logits = jnp.where(same[None], logits, -1e30)
    top = jnp.max(logits, axis=-1, keepdims=True)
    expo = jnp.exp(logits - top)
    weights = (expo / jnp.sum(expo, axis=-1, keepdims=True)).astype(jnp.bfloat16)
    context = jnp.einsum("hts,shd->thd", weights, values, preferred_element_type=jnp.float32)
    context = context.astype(jnp.bfloat16).reshape(tokens_here, local_width)
    partial_value = jnp.dot(context, w_output, preferred_element_type=jnp.float32)
    attended = settle(partial_value, hidden, b_output, first_gain, first_shift, n_tensor)
    activated = jax.nn.gelu(
        jnp.dot(attended, w_up, preferred_element_type=jnp.float32) + b_up, approximate=False
    ).astype(jnp.bfloat16)
    partial_value = jnp.dot(activated, w_down, preferred_element_type=jnp.float32)
    states = settle(partial_value, attended, b_down, second_gain, second_shift, n_tensor)
    texts_here = lengths.shape[1]
    member = (segment[None, :] == jnp.arange(texts_here, dtype=jnp.int32)[:, None]).astype(
        jnp.bfloat16
    )
    pooled = (
        jnp.dot(member, states, preferred_element_type=jnp.float32)
        / lengths[0].astype(jnp.float32)[:, None]
    )
    unit = pooled * lax.rsqrt(jnp.sum(pooled * pooled, axis=-1, keepdims=True) + 1e-06)
    quarter = index.shape[1]
    unit_quarter = lax.dynamic_slice_in_dim(
        unit, lax.axis_index("tensor") * quarter, quarter, 1
    ).astype(jnp.bfloat16)
    row_base = lax.axis_index("dp") * index.shape[0]
    xor_ok = (
        is_power_of_two(n_dp)
        and is_power_of_two(n_tensor)
        and candidates.shape[0] % n_dp == 0
    )
    if xor_ok:
        gathered = all_gather_xor(unit_quarter, "dp", n_dp, levels_of(n_dp))
    else:
        gathered = lax.all_gather(unit_quarter, "dp", axis=0, tiled=True)
    all_texts = candidates.shape[0]
    shard_rows = index.shape[0]
    local_rows = candidates - row_base
    held = (local_rows >= 0) & (local_rows < shard_rows)
    tile = lax.dot_general(
        gathered, index, (((1,), (1,)), ((), ())), preferred_element_type=jnp.float32
    )
    wanted = jnp.clip(local_rows, 0, shard_rows - 1)
    minor = 16
    if shard_rows % minor == 0:
        major = shard_rows // minor
        major_hot = (
            (wanted // minor)[:, :, None] == jnp.arange(major, dtype=jnp.int32)[None, None, :]
        ).astype(jnp.float32)
        rows_of = jnp.einsum(
            "tca,tab->tcb",
            major_hot,
            tile.reshape(all_texts, major, minor),
            precision=lax.Precision.HIGHEST,
            preferred_element_type=jnp.float32,
        )
        minor_hot = (wanted % minor)[:, :, None] == jnp.arange(minor, dtype=jnp.int32)[None, None, :]
        picked = jnp.sum(jnp.where(minor_hot, rows_of, 0.0), axis=2)
    else:
        row_ids = jnp.arange(shard_rows, dtype=jnp.int32)
        chosen = wanted[:, :, None] == row_ids[None, None, :]
        picked = jnp.sum(jnp.where(chosen, tile[:, None, :], 0.0), axis=2)
    partial_scores = jnp.where(held, picked, 0.0)
    if not xor_ok:
        slice_scores = lax.psum_scatter(
            partial_scores, ("dp", "tensor"), scatter_dimension=0, tiled=True
        )
        scores = lax.all_gather(slice_scores, "tensor", axis=0, tiled=True)
        return (states, scores)
    text_scores, _ = reduce_scatter_xor(partial_scores, "dp", n_dp, levels_of(n_dp)[::-1])
    for k in levels_of(n_tensor):
        text_scores = text_scores + lax.ppermute(text_scores, "tensor", xor_pairs(n_tensor, k))
    return (states, text_scores)


def solution(mesh):
    placed = (
        P("dp", None),
        P("dp", None),
        P(None, None, "tensor"),
        P(None, "tensor"),
        P("tensor", None),
        P(),
        P(),
        P(),
        P(None, "tensor"),
        P("tensor"),
        P("tensor", None),
        P(),
        P(),
        P(),
        P("dp", "tensor"),
        P(),
    )
    n_dp = mesh.shape["dp"]
    n_tensor = mesh.shape["tensor"]

    def run(*args):
        return body(*args, n_dp=n_dp, n_tensor=n_tensor)

    return jax.shard_map(
        run, mesh=mesh, in_specs=placed, out_specs=(P("dp", None), P("dp", None)), check_vma=False
    )
```

```python
import math

import jax
import jax.numpy as jnp
from jax import lax
from jax.sharding import PartitionSpec as P

HEAD = 64


def layer_norm(values, gain, shift):
    centre = jnp.mean(values, axis=-1, keepdims=True)
    centred = values - centre
    spread = jnp.mean(centred * centred, axis=-1, keepdims=True)
    return centred * lax.rsqrt(spread + 1e-05) * gain + shift


def segment_of(pack_lengths, count):
    ends = jnp.cumsum(pack_lengths)
    position = jnp.arange(count, dtype=jnp.int32)
    return jnp.sum((position[:, None] >= ends[None, :]).astype(jnp.int32), axis=1)


def is_power_of_two(n):
    return n >= 1 and (n & (n - 1)) == 0


def xor_pairs(n, k):
    return [(i, i ^ k) for i in range(n)]


def levels_of(n):
    return [1 << j for j in range(int(math.log2(n)))] if n > 1 else []


def reduce_scatter_xor(value, axis, n, levels):
    index = lax.axis_index(axis)
    acc = value
    block = 0
    count = 1
    for k in levels:
        half = acc.shape[0] // 2
        bit = (index // k) % 2
        mine = lax.dynamic_slice_in_dim(acc, bit * half, half, 0)
        theirs = lax.dynamic_slice_in_dim(acc, (1 - bit) * half, half, 0)
        wire = jnp.float32 if value.dtype == jnp.float32 else jnp.bfloat16
        got = lax.ppermute(theirs.astype(wire), axis, xor_pairs(n, k))
        acc = mine.astype(jnp.float32) + got.astype(jnp.float32)
        count *= 2
        block = block * 2 + bit
    return acc, block


def all_gather_xor(value, axis, n, levels):
    index = lax.axis_index(axis)
    cur = value
    for k in levels:
        other = lax.ppermute(cur, axis, xor_pairs(n, k))
        bit = (index // k) % 2
        cur = jnp.where(bit == 0, jnp.concatenate([cur, other]), jnp.concatenate([other, cur]))
    return cur


def settle(partial_value, residual, bias, gain, shift, n_tensor):
    if not is_power_of_two(n_tensor) or partial_value.shape[0] % n_tensor:
        total = lax.psum(partial_value.astype(jnp.bfloat16), "tensor").astype(jnp.float32)
        return layer_norm(total + bias + residual.astype(jnp.float32), gain, shift).astype(
            jnp.bfloat16
        )
    levels = levels_of(n_tensor)
    total, block = reduce_scatter_xor(partial_value.astype(jnp.bfloat16), "tensor", n_tensor, levels)
    rows = total.shape[0]
    own_residual = lax.dynamic_slice_in_dim(residual, block * rows, rows, 0)
    normed = layer_norm(total + bias + own_residual.astype(jnp.float32), gain, shift).astype(
        jnp.bfloat16
    )
    return all_gather_xor(normed, "tensor", n_tensor, levels[::-1])


def body(
    hidden,
    lengths,
    w_qkv,
    b_qkv,
    w_output,
    b_output,
    first_gain,
    first_shift,
    w_up,
    b_up,
    w_down,
    b_down,
    second_gain,
    second_shift,
    index,
    candidates,
    n_dp,
    n_tensor,
):
    tokens_here = hidden.shape[0]
    local_width = w_qkv.shape[2]
    local_heads = local_width // HEAD
    projected = [
        jnp.dot(hidden, w_qkv[j], preferred_element_type=jnp.float32) + b_qkv[j] for j in range(3)
    ]
    queries = (projected[0] * 0.125).astype(jnp.bfloat16).reshape(tokens_here, local_heads, HEAD)
    keys = projected[1].astype(jnp.bfloat16).reshape(tokens_here, local_heads, HEAD)
    values = projected[2].astype(jnp.bfloat16).reshape(tokens_here, local_heads, HEAD)
    segment = segment_of(lengths[0], tokens_here)
    same = segment[:, None] == segment[None, :]
    logits = jnp.einsum("thd,shd->hts", queries, keys, preferred_element_type=jnp.float32)
    logits = jnp.where(same[None], logits, -1e30)
    top = jnp.max(logits, axis=-1, keepdims=True)
    expo = jnp.exp(logits - top)
    weights = (expo / jnp.sum(expo, axis=-1, keepdims=True)).astype(jnp.bfloat16)
    context = jnp.einsum("hts,shd->thd", weights, values, preferred_element_type=jnp.float32)
    context = context.astype(jnp.bfloat16).reshape(tokens_here, local_width)
    partial_value = jnp.dot(context, w_output, preferred_element_type=jnp.float32)
    attended = settle(partial_value, hidden, b_output, first_gain, first_shift, n_tensor)
    activated = jax.nn.gelu(
        jnp.dot(attended, w_up, preferred_element_type=jnp.float32) + b_up, approximate=False
    ).astype(jnp.bfloat16)
    partial_value = jnp.dot(activated, w_down, preferred_element_type=jnp.float32)
    states = settle(partial_value, attended, b_down, second_gain, second_shift, n_tensor)
    texts_here = lengths.shape[1]
    member = (segment[None, :] == jnp.arange(texts_here, dtype=jnp.int32)[:, None]).astype(
        jnp.bfloat16
    )
    pooled = (
        jnp.dot(member, states, preferred_element_type=jnp.float32)
        / lengths[0].astype(jnp.float32)[:, None]
    )
    unit = pooled * lax.rsqrt(jnp.sum(pooled * pooled, axis=-1, keepdims=True) + 1e-06)
    quarter = index.shape[1]
    unit_quarter = lax.dynamic_slice_in_dim(
        unit, lax.axis_index("tensor") * quarter, quarter, 1
    ).astype(jnp.bfloat16)
    row_base = lax.axis_index("dp") * index.shape[0]
    xor_ok = (
        is_power_of_two(n_dp)
        and is_power_of_two(n_tensor)
        and candidates.shape[0] % n_dp == 0
    )
    if xor_ok:
        gathered = all_gather_xor(unit_quarter, "dp", n_dp, levels_of(n_dp))
    else:
        gathered = lax.all_gather(unit_quarter, "dp", axis=0, tiled=True)
    all_texts = candidates.shape[0]
    shard_rows = index.shape[0]
    local_rows = candidates - row_base
    held = (local_rows >= 0) & (local_rows < shard_rows)
    tile = lax.dot_general(
        gathered, index, (((1,), (1,)), ((), ())), preferred_element_type=jnp.float32
    )
    wanted = jnp.clip(local_rows, 0, shard_rows - 1)
    minor = 16
    if shard_rows % minor == 0:
        major = shard_rows // minor
        major_hot = (
            (wanted // minor)[:, :, None] == jnp.arange(major, dtype=jnp.int32)[None, None, :]
        ).astype(jnp.bfloat16)
        high = tile.astype(jnp.bfloat16)
        rest = tile - high.astype(jnp.float32)
        middle = rest.astype(jnp.bfloat16)
        low = (rest - middle.astype(jnp.float32)).astype(jnp.bfloat16)
        parts = jnp.concatenate(
            [p.reshape(all_texts, major, minor) for p in (high, middle, low)], axis=2
        )
        chosen_parts = jnp.einsum(
            "tca,tab->tcb", major_hot, parts, preferred_element_type=jnp.float32
        )
        rows_of = (
            chosen_parts[:, :, :minor] + chosen_parts[:, :, minor : 2 * minor]
        ) + chosen_parts[:, :, 2 * minor :]
        minor_hot = (wanted % minor)[:, :, None] == jnp.arange(minor, dtype=jnp.int32)[None, None, :]
        picked = jnp.sum(jnp.where(minor_hot, rows_of, 0.0), axis=2)
    else:
        row_ids = jnp.arange(shard_rows, dtype=jnp.int32)
        chosen = wanted[:, :, None] == row_ids[None, None, :]
        picked = jnp.sum(jnp.where(chosen, tile[:, None, :], 0.0), axis=2)
    partial_scores = jnp.where(held, picked, 0.0)
    if not xor_ok:
        slice_scores = lax.psum_scatter(
            partial_scores, ("dp", "tensor"), scatter_dimension=0, tiled=True
        )
        scores = lax.all_gather(slice_scores, "tensor", axis=0, tiled=True)
        return (states, scores)
    text_scores, _ = reduce_scatter_xor(partial_scores, "dp", n_dp, levels_of(n_dp)[::-1])
    for k in levels_of(n_tensor):
        text_scores = text_scores + lax.ppermute(text_scores, "tensor", xor_pairs(n_tensor, k))
    return (states, text_scores)


def solution(mesh):
    placed = (
        P("dp", None),
        P("dp", None),
        P(None, None, "tensor"),
        P(None, "tensor"),
        P("tensor", None),
        P(),
        P(),
        P(),
        P(None, "tensor"),
        P("tensor"),
        P("tensor", None),
        P(),
        P(),
        P(),
        P("dp", "tensor"),
        P(),
    )
    n_dp = mesh.shape["dp"]
    n_tensor = mesh.shape["tensor"]

    def run(*args):
        return body(*args, n_dp=n_dp, n_tensor=n_tensor)

    return jax.shard_map(
        run, mesh=mesh, in_specs=placed, out_specs=(P("dp", None), P("dp", None)), check_vma=False
    )
```

```python
import math

import jax
import jax.numpy as jnp
from jax import lax
from jax.sharding import PartitionSpec as P

HEAD = 64


def layer_norm(values, gain, shift):
    centre = jnp.mean(values, axis=-1, keepdims=True)
    centred = values - centre
    spread = jnp.mean(centred * centred, axis=-1, keepdims=True)
    return centred * lax.rsqrt(spread + 1e-05) * gain + shift


def segment_of(pack_lengths, count):
    ends = jnp.cumsum(pack_lengths)
    position = jnp.arange(count, dtype=jnp.int32)
    return jnp.sum((position[:, None] >= ends[None, :]).astype(jnp.int32), axis=1)


def is_power_of_two(n):
    return n >= 1 and (n & (n - 1)) == 0


def xor_pairs(n, k):
    return [(i, i ^ k) for i in range(n)]


def levels_of(n):
    return [1 << j for j in range(int(math.log2(n)))] if n > 1 else []


def reduce_scatter_xor(value, axis, n, levels):
    index = lax.axis_index(axis)
    acc = value
    block = 0
    count = 1
    for k in levels:
        half = acc.shape[0] // 2
        bit = (index // k) % 2
        mine = lax.dynamic_slice_in_dim(acc, bit * half, half, 0)
        theirs = lax.dynamic_slice_in_dim(acc, (1 - bit) * half, half, 0)
        wire = jnp.float32 if value.dtype == jnp.float32 else jnp.bfloat16
        got = lax.ppermute(theirs.astype(wire), axis, xor_pairs(n, k))
        acc = mine.astype(jnp.float32) + got.astype(jnp.float32)
        count *= 2
        block = block * 2 + bit
    return acc, block


def all_gather_xor(value, axis, n, levels):
    index = lax.axis_index(axis)
    cur = value
    for k in levels:
        other = lax.ppermute(cur, axis, xor_pairs(n, k))
        bit = (index // k) % 2
        cur = jnp.where(bit == 0, jnp.concatenate([cur, other]), jnp.concatenate([other, cur]))
    return cur


def settle(partial_value, residual, bias, gain, shift, n_tensor):
    if not is_power_of_two(n_tensor) or partial_value.shape[0] % n_tensor:
        total = lax.psum(partial_value.astype(jnp.bfloat16), "tensor").astype(jnp.float32)
        return layer_norm(total + bias + residual.astype(jnp.float32), gain, shift).astype(
            jnp.bfloat16
        )
    levels = levels_of(n_tensor)
    total, block = reduce_scatter_xor(partial_value.astype(jnp.bfloat16), "tensor", n_tensor, levels)
    rows = total.shape[0]
    own_residual = lax.dynamic_slice_in_dim(residual, block * rows, rows, 0)
    normed = layer_norm(total + bias + own_residual.astype(jnp.float32), gain, shift).astype(
        jnp.bfloat16
    )
    return all_gather_xor(normed, "tensor", n_tensor, levels[::-1])


def body(
    hidden,
    lengths,
    w_qkv,
    b_qkv,
    w_output,
    b_output,
    first_gain,
    first_shift,
    w_up,
    b_up,
    w_down,
    b_down,
    second_gain,
    second_shift,
    index,
    candidates,
    n_dp,
    n_tensor,
):
    tokens_here = hidden.shape[0]
    local_width = w_qkv.shape[2]
    local_heads = local_width // HEAD
    projected = [
        jnp.dot(hidden, w_qkv[j], preferred_element_type=jnp.float32) + b_qkv[j] for j in range(3)
    ]
    queries = (projected[0] * 0.125).astype(jnp.bfloat16).reshape(tokens_here, local_heads, HEAD)
    keys = projected[1].astype(jnp.bfloat16).reshape(tokens_here, local_heads, HEAD)
    values = projected[2].astype(jnp.bfloat16).reshape(tokens_here, local_heads, HEAD)
    segment = segment_of(lengths[0], tokens_here)
    same = segment[:, None] == segment[None, :]
    logits = jnp.einsum("thd,shd->hts", queries, keys, preferred_element_type=jnp.float32)
    logits = jnp.where(same[None], logits, -1e30)
    top = jnp.max(logits, axis=-1, keepdims=True)
    expo = jnp.exp(logits - top)
    weights = (expo / jnp.sum(expo, axis=-1, keepdims=True)).astype(jnp.bfloat16)
    context = jnp.einsum("hts,shd->thd", weights, values, preferred_element_type=jnp.float32)
    context = context.astype(jnp.bfloat16).reshape(tokens_here, local_width)
    partial_value = jnp.dot(context, w_output, preferred_element_type=jnp.float32)
    attended = settle(partial_value, hidden, b_output, first_gain, first_shift, n_tensor)
    activated = jax.nn.gelu(
        jnp.dot(attended, w_up, preferred_element_type=jnp.float32) + b_up, approximate=False
    ).astype(jnp.bfloat16)
    partial_value = jnp.dot(activated, w_down, preferred_element_type=jnp.float32)
    states = settle(partial_value, attended, b_down, second_gain, second_shift, n_tensor)
    texts_here = lengths.shape[1]
    member = (segment[None, :] == jnp.arange(texts_here, dtype=jnp.int32)[:, None]).astype(
        jnp.bfloat16
    )
    pooled = (
        jnp.dot(member, states, preferred_element_type=jnp.float32)
        / lengths[0].astype(jnp.float32)[:, None]
    )
    unit = pooled * lax.rsqrt(jnp.sum(pooled * pooled, axis=-1, keepdims=True) + 1e-06)
    quarter = index.shape[1]
    unit_quarter = lax.dynamic_slice_in_dim(
        unit, lax.axis_index("tensor") * quarter, quarter, 1
    ).astype(jnp.bfloat16)
    row_base = lax.axis_index("dp") * index.shape[0]
    xor_ok = (
        is_power_of_two(n_dp)
        and is_power_of_two(n_tensor)
        and candidates.shape[0] % n_dp == 0
    )
    if xor_ok:
        gathered = all_gather_xor(unit_quarter, "dp", n_dp, levels_of(n_dp))
    else:
        gathered = lax.all_gather(unit_quarter, "dp", axis=0, tiled=True)
    all_texts = candidates.shape[0]
    shard_rows = index.shape[0]
    local_rows = candidates - row_base
    held = (local_rows >= 0) & (local_rows < shard_rows)
    tile = lax.dot_general(
        gathered, index, (((1,), (1,)), ((), ())), preferred_element_type=jnp.float32
    )
    wanted = jnp.clip(local_rows, 0, shard_rows - 1)
    minor = 128
    if shard_rows % minor == 0:
        major = shard_rows // minor
        major_hot = (
            (wanted // minor)[:, :, None] == jnp.arange(major, dtype=jnp.int32)[None, None, :]
        ).astype(jnp.float32)
        rows_of = jnp.einsum(
            "tca,tab->tcb",
            major_hot,
            tile.reshape(all_texts, major, minor),
            precision=lax.Precision.HIGHEST,
            preferred_element_type=jnp.float32,
        )
        minor_hot = (wanted % minor)[:, :, None] == jnp.arange(minor, dtype=jnp.int32)[None, None, :]
        picked = jnp.sum(jnp.where(minor_hot, rows_of, 0.0), axis=2)
    else:
        row_ids = jnp.arange(shard_rows, dtype=jnp.int32)
        chosen = wanted[:, :, None] == row_ids[None, None, :]
        picked = jnp.sum(jnp.where(chosen, tile[:, None, :], 0.0), axis=2)
    partial_scores = jnp.where(held, picked, 0.0)
    if not xor_ok:
        slice_scores = lax.psum_scatter(
            partial_scores, ("dp", "tensor"), scatter_dimension=0, tiled=True
        )
        scores = lax.all_gather(slice_scores, "tensor", axis=0, tiled=True)
        return (states, scores)
    text_scores, _ = reduce_scatter_xor(partial_scores, "dp", n_dp, levels_of(n_dp)[::-1])
    for k in levels_of(n_tensor):
        text_scores = text_scores + lax.ppermute(text_scores, "tensor", xor_pairs(n_tensor, k))
    return (states, text_scores)


def solution(mesh):
    placed = (
        P("dp", None),
        P("dp", None),
        P(None, None, "tensor"),
        P(None, "tensor"),
        P("tensor", None),
        P(),
        P(),
        P(),
        P(None, "tensor"),
        P("tensor"),
        P("tensor", None),
        P(),
        P(),
        P(),
        P("dp", "tensor"),
        P(),
    )
    n_dp = mesh.shape["dp"]
    n_tensor = mesh.shape["tensor"]

    def run(*args):
        return body(*args, n_dp=n_dp, n_tensor=n_tensor)

    return jax.shard_map(
        run, mesh=mesh, in_specs=placed, out_specs=(P("dp", None), P("dp", None)), check_vma=False
    )
```

```python
import math

import jax
import jax.numpy as jnp
from jax import lax
from jax.sharding import PartitionSpec as P

HEAD = 64


def layer_norm(values, gain, shift):
    centre = jnp.mean(values, axis=-1, keepdims=True)
    centred = values - centre
    spread = jnp.mean(centred * centred, axis=-1, keepdims=True)
    return centred * lax.rsqrt(spread + 1e-05) * gain + shift


def segment_of(pack_lengths, count):
    ends = jnp.cumsum(pack_lengths)
    position = jnp.arange(count, dtype=jnp.int32)
    return jnp.sum((position[:, None] >= ends[None, :]).astype(jnp.int32), axis=1)


def is_power_of_two(n):
    return n >= 1 and (n & (n - 1)) == 0


def xor_pairs(n, k):
    return [(i, i ^ k) for i in range(n)]


def levels_of(n):
    return [1 << j for j in range(int(math.log2(n)))] if n > 1 else []


def reduce_scatter_xor(value, axis, n, levels):
    index = lax.axis_index(axis)
    acc = value
    block = 0
    count = 1
    for k in levels:
        half = acc.shape[0] // 2
        bit = (index // k) % 2
        mine = lax.dynamic_slice_in_dim(acc, bit * half, half, 0)
        theirs = lax.dynamic_slice_in_dim(acc, (1 - bit) * half, half, 0)
        wire = jnp.float32 if value.dtype == jnp.float32 else jnp.bfloat16
        got = lax.ppermute(theirs.astype(wire), axis, xor_pairs(n, k))
        acc = mine.astype(jnp.float32) + got.astype(jnp.float32)
        count *= 2
        block = block * 2 + bit
    return acc, block


def all_gather_xor(value, axis, n, levels):
    index = lax.axis_index(axis)
    cur = value
    for k in levels:
        other = lax.ppermute(cur, axis, xor_pairs(n, k))
        bit = (index // k) % 2
        cur = jnp.where(bit == 0, jnp.concatenate([cur, other]), jnp.concatenate([other, cur]))
    return cur


def settle(partial_value, residual, bias, gain, shift, n_tensor):
    if not is_power_of_two(n_tensor) or partial_value.shape[0] % n_tensor:
        total = lax.psum(partial_value.astype(jnp.bfloat16), "tensor").astype(jnp.float32)
        return layer_norm(total + bias + residual.astype(jnp.float32), gain, shift).astype(
            jnp.bfloat16
        )
    levels = levels_of(n_tensor)
    total, block = reduce_scatter_xor(partial_value.astype(jnp.bfloat16), "tensor", n_tensor, levels)
    rows = total.shape[0]
    own_residual = lax.dynamic_slice_in_dim(residual, block * rows, rows, 0)
    normed = layer_norm(total + bias + own_residual.astype(jnp.float32), gain, shift).astype(
        jnp.bfloat16
    )
    return all_gather_xor(normed, "tensor", n_tensor, levels[::-1])


def body(
    hidden,
    lengths,
    w_qkv,
    b_qkv,
    w_output,
    b_output,
    first_gain,
    first_shift,
    w_up,
    b_up,
    w_down,
    b_down,
    second_gain,
    second_shift,
    index,
    candidates,
    n_dp,
    n_tensor,
):
    tokens_here = hidden.shape[0]
    local_width = w_qkv.shape[2]
    local_heads = local_width // HEAD
    projected = (
        jnp.einsum("td,jdf->jtf", hidden, w_qkv, preferred_element_type=jnp.float32)
        + b_qkv[:, None, :]
    )
    queries = (projected[0] * 0.125).astype(jnp.bfloat16).reshape(tokens_here, local_heads, HEAD)
    keys = projected[1].astype(jnp.bfloat16).reshape(tokens_here, local_heads, HEAD)
    values = projected[2].astype(jnp.bfloat16).reshape(tokens_here, local_heads, HEAD)
    segment = segment_of(lengths[0], tokens_here)
    same = segment[:, None] == segment[None, :]
    logits = jnp.einsum("thd,shd->hts", queries, keys, preferred_element_type=jnp.float32)
    logits = jnp.where(same[None], logits, -1e30)
    top = jnp.max(logits, axis=-1, keepdims=True)
    expo = jnp.exp(logits - top)
    weights = (expo / jnp.sum(expo, axis=-1, keepdims=True)).astype(jnp.bfloat16)
    context = jnp.einsum("hts,shd->thd", weights, values, preferred_element_type=jnp.float32)
    context = context.astype(jnp.bfloat16).reshape(tokens_here, local_width)
    partial_value = jnp.dot(context, w_output, preferred_element_type=jnp.float32)
    attended = settle(partial_value, hidden, b_output, first_gain, first_shift, n_tensor)
    activated = jax.nn.gelu(
        jnp.dot(attended, w_up, preferred_element_type=jnp.float32) + b_up, approximate=False
    ).astype(jnp.bfloat16)
    partial_value = jnp.dot(activated, w_down, preferred_element_type=jnp.float32)
    states = settle(partial_value, attended, b_down, second_gain, second_shift, n_tensor)
    texts_here = lengths.shape[1]
    member = (segment[None, :] == jnp.arange(texts_here, dtype=jnp.int32)[:, None]).astype(
        jnp.bfloat16
    )
    pooled = (
        jnp.dot(member, states, preferred_element_type=jnp.float32)
        / lengths[0].astype(jnp.float32)[:, None]
    )
    unit = pooled * lax.rsqrt(jnp.sum(pooled * pooled, axis=-1, keepdims=True) + 1e-06)
    quarter = index.shape[1]
    unit_quarter = lax.dynamic_slice_in_dim(
        unit, lax.axis_index("tensor") * quarter, quarter, 1
    ).astype(jnp.bfloat16)
    row_base = lax.axis_index("dp") * index.shape[0]
    xor_ok = (
        is_power_of_two(n_dp)
        and is_power_of_two(n_tensor)
        and candidates.shape[0] % n_dp == 0
    )
    if xor_ok:
        gathered = all_gather_xor(unit_quarter, "dp", n_dp, levels_of(n_dp))
    else:
        gathered = lax.all_gather(unit_quarter, "dp", axis=0, tiled=True)
    all_texts = candidates.shape[0]
    shard_rows = index.shape[0]
    local_rows = candidates - row_base
    held = (local_rows >= 0) & (local_rows < shard_rows)
    tile = lax.dot_general(
        gathered, index, (((1,), (1,)), ((), ())), preferred_element_type=jnp.float32
    )
    wanted = jnp.clip(local_rows, 0, shard_rows - 1)
    minor = 128
    if shard_rows % minor == 0:
        major = shard_rows // minor
        major_hot = (
            (wanted // minor)[:, :, None] == jnp.arange(major, dtype=jnp.int32)[None, None, :]
        ).astype(jnp.float32)
        rows_of = jnp.einsum(
            "tca,tab->tcb",
            major_hot,
            tile.reshape(all_texts, major, minor),
            precision=lax.Precision.HIGHEST,
            preferred_element_type=jnp.float32,
        )
        minor_hot = (wanted % minor)[:, :, None] == jnp.arange(minor, dtype=jnp.int32)[None, None, :]
        picked = jnp.sum(jnp.where(minor_hot, rows_of, 0.0), axis=2)
    else:
        row_ids = jnp.arange(shard_rows, dtype=jnp.int32)
        chosen = wanted[:, :, None] == row_ids[None, None, :]
        picked = jnp.sum(jnp.where(chosen, tile[:, None, :], 0.0), axis=2)
    partial_scores = jnp.where(held, picked, 0.0)
    if not xor_ok:
        slice_scores = lax.psum_scatter(
            partial_scores, ("dp", "tensor"), scatter_dimension=0, tiled=True
        )
        scores = lax.all_gather(slice_scores, "tensor", axis=0, tiled=True)
        return (states, scores)
    text_scores, _ = reduce_scatter_xor(partial_scores, "dp", n_dp, levels_of(n_dp)[::-1])
    for k in levels_of(n_tensor):
        text_scores = text_scores + lax.ppermute(text_scores, "tensor", xor_pairs(n_tensor, k))
    return (states, text_scores)


def solution(mesh):
    placed = (
        P("dp", None),
        P("dp", None),
        P(None, None, "tensor"),
        P(None, "tensor"),
        P("tensor", None),
        P(),
        P(),
        P(),
        P(None, "tensor"),
        P("tensor"),
        P("tensor", None),
        P(),
        P(),
        P(),
        P("dp", "tensor"),
        P(),
    )
    n_dp = mesh.shape["dp"]
    n_tensor = mesh.shape["tensor"]

    def run(*args):
        return body(*args, n_dp=n_dp, n_tensor=n_tensor)

    return jax.shard_map(
        run, mesh=mesh, in_specs=placed, out_specs=(P("dp", None), P("dp", None)), check_vma=False
    )
```

```python
import math

import jax
import jax.numpy as jnp
from jax import lax
from jax.sharding import PartitionSpec as P

HEAD = 64


def layer_norm(values, gain, shift):
    centre = jnp.mean(values, axis=-1, keepdims=True)
    centred = values - centre
    spread = jnp.mean(centred * centred, axis=-1, keepdims=True)
    return centred * lax.rsqrt(spread + 1e-05) * gain + shift


def segment_of(pack_lengths, count):
    ends = jnp.cumsum(pack_lengths)
    position = jnp.arange(count, dtype=jnp.int32)
    return jnp.sum((position[:, None] >= ends[None, :]).astype(jnp.int32), axis=1)


def is_power_of_two(n):
    return n >= 1 and (n & (n - 1)) == 0


def xor_pairs(n, k):
    return [(i, i ^ k) for i in range(n)]


def levels_of(n):
    return [1 << j for j in range(int(math.log2(n)))] if n > 1 else []


def reduce_scatter_xor(value, axis, n, levels):
    index = lax.axis_index(axis)
    acc = value
    block = 0
    count = 1
    for k in levels:
        half = acc.shape[0] // 2
        bit = (index // k) % 2
        mine = lax.dynamic_slice_in_dim(acc, bit * half, half, 0)
        theirs = lax.dynamic_slice_in_dim(acc, (1 - bit) * half, half, 0)
        wire = jnp.float32 if value.dtype == jnp.float32 else jnp.bfloat16
        got = lax.ppermute(theirs.astype(wire), axis, xor_pairs(n, k))
        acc = mine.astype(jnp.float32) + got.astype(jnp.float32)
        count *= 2
        block = block * 2 + bit
    return acc, block


def all_gather_xor(value, axis, n, levels):
    index = lax.axis_index(axis)
    cur = value
    for k in levels:
        other = lax.ppermute(cur, axis, xor_pairs(n, k))
        bit = (index // k) % 2
        cur = jnp.where(bit == 0, jnp.concatenate([cur, other]), jnp.concatenate([other, cur]))
    return cur


def settle(partial_value, residual, bias, gain, shift, n_tensor):
    if not is_power_of_two(n_tensor) or partial_value.shape[0] % n_tensor:
        total = lax.psum(partial_value.astype(jnp.bfloat16), "tensor").astype(jnp.float32)
        return layer_norm(total + bias + residual.astype(jnp.float32), gain, shift).astype(
            jnp.bfloat16
        )
    levels = levels_of(n_tensor)
    total, block = reduce_scatter_xor(partial_value.astype(jnp.bfloat16), "tensor", n_tensor, levels)
    rows = total.shape[0]
    own_residual = lax.dynamic_slice_in_dim(residual, block * rows, rows, 0)
    normed = layer_norm(total + bias + own_residual.astype(jnp.float32), gain, shift).astype(
        jnp.bfloat16
    )
    return all_gather_xor(normed, "tensor", n_tensor, levels[::-1])


def in_order(first_bit, mine, other):
    return jnp.where(first_bit == 0, jnp.concatenate([mine, other]), jnp.concatenate([other, mine]))


def overlapped_layer(
    partial_value, hidden, b_output, first_gain, first_shift, feed_forward, b_down, second_gain,
    second_shift,
):
    index = lax.axis_index("tensor")
    low = index % 2
    high = (index // 2) % 2
    total, block = reduce_scatter_xor(partial_value.astype(jnp.bfloat16), "tensor", 4, [1, 2])
    rows = total.shape[0]
    own_residual = lax.dynamic_slice_in_dim(hidden, block * rows, rows, 0)
    own = layer_norm(total + b_output + own_residual.astype(jnp.float32), first_gain, first_shift)
    own = own.astype(jnp.bfloat16)
    cross = lax.ppermute(own, "tensor", xor_pairs(4, 2))
    own_out = feed_forward(own)
    half = in_order(high, own, cross)
    other_half = lax.ppermute(half, "tensor", xor_pairs(4, 1))
    cross_out = feed_forward(cross)
    other_out = feed_forward(other_half)
    got = lax.ppermute(other_out.astype(jnp.bfloat16), "tensor", xor_pairs(4, 1))
    half_sum = in_order(high, own_out, cross_out) + got.astype(jnp.float32)
    keep = lax.dynamic_slice_in_dim(half_sum, high * rows, rows, 0)
    send = lax.dynamic_slice_in_dim(half_sum, (1 - high) * rows, rows, 0)
    got = lax.ppermute(send.astype(jnp.bfloat16), "tensor", xor_pairs(4, 2))
    total = keep + got.astype(jnp.float32)
    normed = layer_norm(total + b_down + own.astype(jnp.float32), second_gain, second_shift)
    return all_gather_xor(normed.astype(jnp.bfloat16), "tensor", 4, [2, 1])


def body(
    hidden,
    lengths,
    w_qkv,
    b_qkv,
    w_output,
    b_output,
    first_gain,
    first_shift,
    w_up,
    b_up,
    w_down,
    b_down,
    second_gain,
    second_shift,
    index,
    candidates,
    n_dp,
    n_tensor,
):
    tokens_here = hidden.shape[0]
    local_width = w_qkv.shape[2]
    local_heads = local_width // HEAD
    projected = (
        jnp.einsum("td,jdf->jtf", hidden, w_qkv, preferred_element_type=jnp.float32)
        + b_qkv[:, None, :]
    )
    queries = (projected[0] * 0.125).astype(jnp.bfloat16).reshape(tokens_here, local_heads, HEAD)
    keys = projected[1].astype(jnp.bfloat16).reshape(tokens_here, local_heads, HEAD)
    values = projected[2].astype(jnp.bfloat16).reshape(tokens_here, local_heads, HEAD)
    segment = segment_of(lengths[0], tokens_here)
    same = segment[:, None] == segment[None, :]
    logits = jnp.einsum("thd,shd->hts", queries, keys, preferred_element_type=jnp.float32)
    logits = jnp.where(same[None], logits, -1e30)
    top = jnp.max(logits, axis=-1, keepdims=True)
    expo = jnp.exp(logits - top)
    weights = (expo / jnp.sum(expo, axis=-1, keepdims=True)).astype(jnp.bfloat16)
    context = jnp.einsum("hts,shd->thd", weights, values, preferred_element_type=jnp.float32)
    context = context.astype(jnp.bfloat16).reshape(tokens_here, local_width)
    partial_value = jnp.dot(context, w_output, preferred_element_type=jnp.float32)
    def feed_forward(rows):
        activated = jax.nn.gelu(
            jnp.dot(rows, w_up, preferred_element_type=jnp.float32) + b_up, approximate=False
        ).astype(jnp.bfloat16)
        return jnp.dot(activated, w_down, preferred_element_type=jnp.float32)

    if n_tensor == 4 and tokens_here % 4 == 0:
        states = overlapped_layer(
            partial_value,
            hidden,
            b_output,
            first_gain,
            first_shift,
            feed_forward,
            b_down,
            second_gain,
            second_shift,
        )
    else:
        attended = settle(partial_value, hidden, b_output, first_gain, first_shift, n_tensor)
        states = settle(
            feed_forward(attended), attended, b_down, second_gain, second_shift, n_tensor
        )
    texts_here = lengths.shape[1]
    member = (segment[None, :] == jnp.arange(texts_here, dtype=jnp.int32)[:, None]).astype(
        jnp.bfloat16
    )
    pooled = (
        jnp.dot(member, states, preferred_element_type=jnp.float32)
        / lengths[0].astype(jnp.float32)[:, None]
    )
    unit = pooled * lax.rsqrt(jnp.sum(pooled * pooled, axis=-1, keepdims=True) + 1e-06)
    quarter = index.shape[1]
    unit_quarter = lax.dynamic_slice_in_dim(
        unit, lax.axis_index("tensor") * quarter, quarter, 1
    ).astype(jnp.bfloat16)
    row_base = lax.axis_index("dp") * index.shape[0]
    xor_ok = (
        is_power_of_two(n_dp)
        and is_power_of_two(n_tensor)
        and candidates.shape[0] % n_dp == 0
    )
    if xor_ok:
        gathered = all_gather_xor(unit_quarter, "dp", n_dp, levels_of(n_dp))
    else:
        gathered = lax.all_gather(unit_quarter, "dp", axis=0, tiled=True)
    all_texts = candidates.shape[0]
    shard_rows = index.shape[0]
    local_rows = candidates - row_base
    held = (local_rows >= 0) & (local_rows < shard_rows)
    tile = lax.dot_general(
        gathered, index, (((1,), (1,)), ((), ())), preferred_element_type=jnp.float32
    )
    wanted = jnp.clip(local_rows, 0, shard_rows - 1)
    minor = 128
    if shard_rows % minor == 0:
        major = shard_rows // minor
        major_hot = (
            (wanted // minor)[:, :, None] == jnp.arange(major, dtype=jnp.int32)[None, None, :]
        ).astype(jnp.float32)
        rows_of = jnp.einsum(
            "tca,tab->tcb",
            major_hot,
            tile.reshape(all_texts, major, minor),
            precision=lax.Precision.HIGHEST,
            preferred_element_type=jnp.float32,
        )
        minor_hot = (wanted % minor)[:, :, None] == jnp.arange(minor, dtype=jnp.int32)[None, None, :]
        picked = jnp.sum(jnp.where(minor_hot, rows_of, 0.0), axis=2)
    else:
        row_ids = jnp.arange(shard_rows, dtype=jnp.int32)
        chosen = wanted[:, :, None] == row_ids[None, None, :]
        picked = jnp.sum(jnp.where(chosen, tile[:, None, :], 0.0), axis=2)
    partial_scores = jnp.where(held, picked, 0.0)
    if not xor_ok:
        slice_scores = lax.psum_scatter(
            partial_scores, ("dp", "tensor"), scatter_dimension=0, tiled=True
        )
        scores = lax.all_gather(slice_scores, "tensor", axis=0, tiled=True)
        return (states, scores)
    text_scores, _ = reduce_scatter_xor(partial_scores, "dp", n_dp, levels_of(n_dp)[::-1])
    for k in levels_of(n_tensor):
        text_scores = text_scores + lax.ppermute(text_scores, "tensor", xor_pairs(n_tensor, k))
    return (states, text_scores)


def solution(mesh):
    placed = (
        P("dp", None),
        P("dp", None),
        P(None, None, "tensor"),
        P(None, "tensor"),
        P("tensor", None),
        P(),
        P(),
        P(),
        P(None, "tensor"),
        P("tensor"),
        P("tensor", None),
        P(),
        P(),
        P(),
        P("dp", "tensor"),
        P(),
    )
    n_dp = mesh.shape["dp"]
    n_tensor = mesh.shape["tensor"]

    def run(*args):
        return body(*args, n_dp=n_dp, n_tensor=n_tensor)

    return jax.shard_map(
        run, mesh=mesh, in_specs=placed, out_specs=(P("dp", None), P("dp", None)), check_vma=False
    )
```

```python
import math

import jax
import jax.numpy as jnp
from jax import lax
from jax.sharding import PartitionSpec as P

HEAD = 64


def layer_norm(values, gain, shift):
    centre = jnp.mean(values, axis=-1, keepdims=True)
    centred = values - centre
    spread = jnp.mean(centred * centred, axis=-1, keepdims=True)
    return centred * lax.rsqrt(spread + 1e-05) * gain + shift


def segment_of(pack_lengths, count):
    ends = jnp.cumsum(pack_lengths)
    position = jnp.arange(count, dtype=jnp.int32)
    return jnp.sum((position[:, None] >= ends[None, :]).astype(jnp.int32), axis=1)


def is_power_of_two(n):
    return n >= 1 and (n & (n - 1)) == 0


def xor_pairs(n, k):
    return [(i, i ^ k) for i in range(n)]


def levels_of(n):
    return [1 << j for j in range(int(math.log2(n)))] if n > 1 else []


def reduce_scatter_xor(value, axis, n, levels):
    index = lax.axis_index(axis)
    acc = value
    block = 0
    count = 1
    for k in levels:
        half = acc.shape[0] // 2
        bit = (index // k) % 2
        mine = lax.dynamic_slice_in_dim(acc, bit * half, half, 0)
        theirs = lax.dynamic_slice_in_dim(acc, (1 - bit) * half, half, 0)
        wire = jnp.float32 if value.dtype == jnp.float32 else jnp.bfloat16
        got = lax.ppermute(theirs.astype(wire), axis, xor_pairs(n, k))
        acc = mine.astype(jnp.float32) + got.astype(jnp.float32)
        count *= 2
        block = block * 2 + bit
    return acc, block


def all_gather_xor(value, axis, n, levels):
    index = lax.axis_index(axis)
    cur = value
    for k in levels:
        other = lax.ppermute(cur, axis, xor_pairs(n, k))
        bit = (index // k) % 2
        cur = jnp.where(bit == 0, jnp.concatenate([cur, other]), jnp.concatenate([other, cur]))
    return cur


def settle(partial_value, residual, bias, gain, shift, n_tensor):
    if not is_power_of_two(n_tensor) or partial_value.shape[0] % n_tensor:
        total = lax.psum(partial_value.astype(jnp.bfloat16), "tensor").astype(jnp.float32)
        return layer_norm(total + bias + residual.astype(jnp.float32), gain, shift).astype(
            jnp.bfloat16
        )
    levels = levels_of(n_tensor)
    total, block = reduce_scatter_xor(partial_value.astype(jnp.bfloat16), "tensor", n_tensor, levels)
    rows = total.shape[0]
    own_residual = lax.dynamic_slice_in_dim(residual, block * rows, rows, 0)
    normed = layer_norm(total + bias + own_residual.astype(jnp.float32), gain, shift).astype(
        jnp.bfloat16
    )
    return all_gather_xor(normed, "tensor", n_tensor, levels[::-1])


def body(
    hidden,
    lengths,
    w_qkv,
    b_qkv,
    w_output,
    b_output,
    first_gain,
    first_shift,
    w_up,
    b_up,
    w_down,
    b_down,
    second_gain,
    second_shift,
    index,
    candidates,
    n_dp,
    n_tensor,
):
    tokens_here = hidden.shape[0]
    local_width = w_qkv.shape[2]
    local_heads = local_width // HEAD
    projected = (
        jnp.einsum("td,jdf->jtf", hidden, w_qkv, preferred_element_type=jnp.float32)
        + b_qkv[:, None, :]
    )
    queries = (projected[0] * 0.125).astype(jnp.bfloat16).reshape(tokens_here, local_heads, HEAD)
    keys = projected[1].astype(jnp.bfloat16).reshape(tokens_here, local_heads, HEAD)
    values = projected[2].astype(jnp.bfloat16).reshape(tokens_here, local_heads, HEAD)
    segment = segment_of(lengths[0], tokens_here)
    same = segment[:, None] == segment[None, :]
    logits = jnp.einsum("thd,shd->hts", queries, keys, preferred_element_type=jnp.float32)
    logits = jnp.where(same[None], logits, -1e30)
    top = jnp.max(logits, axis=-1, keepdims=True)
    expo = jnp.exp(logits - top)
    weights = (expo / jnp.sum(expo, axis=-1, keepdims=True)).astype(jnp.bfloat16)
    context = jnp.einsum("hts,shd->thd", weights, values, preferred_element_type=jnp.float32)
    context = context.astype(jnp.bfloat16).reshape(tokens_here, local_width)
    partial_value = jnp.dot(context, w_output, preferred_element_type=jnp.float32)
    attended = settle(partial_value, hidden, b_output, first_gain, first_shift, n_tensor)
    activated = jax.nn.gelu(
        jnp.dot(attended, w_up, preferred_element_type=jnp.float32) + b_up, approximate=False
    ).astype(jnp.bfloat16)
    partial_value = jnp.dot(activated, w_down, preferred_element_type=jnp.float32)
    states = settle(partial_value, attended, b_down, second_gain, second_shift, n_tensor)
    texts_here = lengths.shape[1]
    member = (segment[None, :] == jnp.arange(texts_here, dtype=jnp.int32)[:, None]).astype(
        jnp.bfloat16
    )
    pooled = (
        jnp.dot(member, states, preferred_element_type=jnp.float32)
        / lengths[0].astype(jnp.float32)[:, None]
    )
    unit = pooled * lax.rsqrt(jnp.sum(pooled * pooled, axis=-1, keepdims=True) + 1e-06)
    quarter = index.shape[1]
    unit_quarter = lax.dynamic_slice_in_dim(
        unit, lax.axis_index("tensor") * quarter, quarter, 1
    ).astype(jnp.bfloat16)
    row_base = lax.axis_index("dp") * index.shape[0]
    xor_ok = (
        is_power_of_two(n_dp)
        and is_power_of_two(n_tensor)
        and candidates.shape[0] % n_dp == 0
    )
    if xor_ok:
        gathered = all_gather_xor(unit_quarter, "dp", n_dp, levels_of(n_dp))
    else:
        gathered = lax.all_gather(unit_quarter, "dp", axis=0, tiled=True)
    all_texts = candidates.shape[0]
    shard_rows = index.shape[0]
    local_rows = candidates - row_base
    held = (local_rows >= 0) & (local_rows < shard_rows)
    tile = lax.dot_general(
        gathered, index, (((1,), (1,)), ((), ())), preferred_element_type=jnp.float32
    )
    wanted = jnp.clip(local_rows, 0, shard_rows - 1)
    minor = 128
    if shard_rows % minor == 0:
        major = shard_rows // minor
        major_hot = (
            (wanted // minor)[:, :, None] == jnp.arange(major, dtype=jnp.int32)[None, None, :]
        ).astype(jnp.float32)
        rows_of = jnp.einsum(
            "tca,tab->tcb",
            major_hot,
            tile.reshape(all_texts, major, minor),
            precision=lax.Precision.HIGH,
            preferred_element_type=jnp.float32,
        )
        minor_hot = (wanted % minor)[:, :, None] == jnp.arange(minor, dtype=jnp.int32)[None, None, :]
        picked = jnp.sum(jnp.where(minor_hot, rows_of, 0.0), axis=2)
    else:
        row_ids = jnp.arange(shard_rows, dtype=jnp.int32)
        chosen = wanted[:, :, None] == row_ids[None, None, :]
        picked = jnp.sum(jnp.where(chosen, tile[:, None, :], 0.0), axis=2)
    partial_scores = jnp.where(held, picked, 0.0)
    if not xor_ok:
        slice_scores = lax.psum_scatter(
            partial_scores, ("dp", "tensor"), scatter_dimension=0, tiled=True
        )
        scores = lax.all_gather(slice_scores, "tensor", axis=0, tiled=True)
        return (states, scores)
    text_scores, _ = reduce_scatter_xor(partial_scores, "dp", n_dp, levels_of(n_dp)[::-1])
    for k in levels_of(n_tensor):
        text_scores = text_scores + lax.ppermute(text_scores, "tensor", xor_pairs(n_tensor, k))
    return (states, text_scores)


def solution(mesh):
    placed = (
        P("dp", None),
        P("dp", None),
        P(None, None, "tensor"),
        P(None, "tensor"),
        P("tensor", None),
        P(),
        P(),
        P(),
        P(None, "tensor"),
        P("tensor"),
        P("tensor", None),
        P(),
        P(),
        P(),
        P("dp", "tensor"),
        P(),
    )
    n_dp = mesh.shape["dp"]
    n_tensor = mesh.shape["tensor"]

    def run(*args):
        return body(*args, n_dp=n_dp, n_tensor=n_tensor)

    return jax.shard_map(
        run, mesh=mesh, in_specs=placed, out_specs=(P("dp", None), P("dp", None)), check_vma=False
    )
```

```python
import math

import jax
import jax.numpy as jnp
from jax import lax
from jax.sharding import PartitionSpec as P

HEAD = 64


def layer_norm(values, gain, shift):
    centre = jnp.mean(values, axis=-1, keepdims=True)
    centred = values - centre
    spread = jnp.mean(centred * centred, axis=-1, keepdims=True)
    return centred * lax.rsqrt(spread + 1e-05) * gain + shift


def segment_of(pack_lengths, count):
    ends = jnp.cumsum(pack_lengths)
    position = jnp.arange(count, dtype=jnp.int32)
    return jnp.sum((position[:, None] >= ends[None, :]).astype(jnp.int32), axis=1)


def is_power_of_two(n):
    return n >= 1 and (n & (n - 1)) == 0


def xor_pairs(n, k):
    return [(i, i ^ k) for i in range(n)]


def levels_of(n):
    return [1 << j for j in range(int(math.log2(n)))] if n > 1 else []


def reduce_scatter_xor(value, axis, n, levels):
    index = lax.axis_index(axis)
    acc = value
    block = 0
    count = 1
    for k in levels:
        half = acc.shape[0] // 2
        bit = (index // k) % 2
        mine = lax.dynamic_slice_in_dim(acc, bit * half, half, 0)
        theirs = lax.dynamic_slice_in_dim(acc, (1 - bit) * half, half, 0)
        wire = jnp.float32 if value.dtype == jnp.float32 else jnp.bfloat16
        got = lax.ppermute(theirs.astype(wire), axis, xor_pairs(n, k))
        acc = mine.astype(jnp.float32) + got.astype(jnp.float32)
        count *= 2
        block = block * 2 + bit
    return acc, block


def all_gather_xor(value, axis, n, levels):
    index = lax.axis_index(axis)
    cur = value
    for k in levels:
        other = lax.ppermute(cur, axis, xor_pairs(n, k))
        bit = (index // k) % 2
        cur = jnp.where(bit == 0, jnp.concatenate([cur, other]), jnp.concatenate([other, cur]))
    return cur


def settle(partial_value, residual, bias, gain, shift, n_tensor):
    if n_tensor == 4 and partial_value.shape[0] % 2 == 0:
        return settle_by_chip(partial_value, residual, bias, gain, shift)
    if not is_power_of_two(n_tensor) or partial_value.shape[0] % n_tensor:
        total = lax.psum(partial_value.astype(jnp.bfloat16), "tensor").astype(jnp.float32)
        return layer_norm(total + bias + residual.astype(jnp.float32), gain, shift).astype(
            jnp.bfloat16
        )
    levels = levels_of(n_tensor)
    total, block = reduce_scatter_xor(partial_value.astype(jnp.bfloat16), "tensor", n_tensor, levels)
    rows = total.shape[0]
    own_residual = lax.dynamic_slice_in_dim(residual, block * rows, rows, 0)
    normed = layer_norm(total + bias + own_residual.astype(jnp.float32), gain, shift).astype(
        jnp.bfloat16
    )
    return all_gather_xor(normed, "tensor", n_tensor, levels[::-1])


def settle_by_chip(partial_value, residual, bias, gain, shift):
    index = lax.axis_index("tensor")
    low = index % 2
    half = partial_value.shape[0] // 2
    rounded = partial_value.astype(jnp.bfloat16)
    mine = lax.dynamic_slice_in_dim(rounded, low * half, half, 0)
    theirs = lax.dynamic_slice_in_dim(rounded, (1 - low) * half, half, 0)
    got = lax.ppermute(theirs, "tensor", xor_pairs(4, 1))
    chip_sum = (mine.astype(jnp.float32) + got.astype(jnp.float32)).astype(jnp.bfloat16)
    across = lax.ppermute(chip_sum, "tensor", xor_pairs(4, 2))
    total = chip_sum.astype(jnp.float32) + across.astype(jnp.float32)
    own_residual = lax.dynamic_slice_in_dim(residual, low * half, half, 0)
    normed = layer_norm(total + bias + own_residual.astype(jnp.float32), gain, shift).astype(
        jnp.bfloat16
    )
    other = lax.ppermute(normed, "tensor", xor_pairs(4, 1))
    return jnp.where(low == 0, jnp.concatenate([normed, other]), jnp.concatenate([other, normed]))


def body(
    hidden,
    lengths,
    w_qkv,
    b_qkv,
    w_output,
    b_output,
    first_gain,
    first_shift,
    w_up,
    b_up,
    w_down,
    b_down,
    second_gain,
    second_shift,
    index,
    candidates,
    n_dp,
    n_tensor,
):
    tokens_here = hidden.shape[0]
    local_width = w_qkv.shape[2]
    local_heads = local_width // HEAD
    projected = (
        jnp.einsum("td,jdf->jtf", hidden, w_qkv, preferred_element_type=jnp.float32)
        + b_qkv[:, None, :]
    )
    queries = (projected[0] * 0.125).astype(jnp.bfloat16).reshape(tokens_here, local_heads, HEAD)
    keys = projected[1].astype(jnp.bfloat16).reshape(tokens_here, local_heads, HEAD)
    values = projected[2].astype(jnp.bfloat16).reshape(tokens_here, local_heads, HEAD)
    segment = segment_of(lengths[0], tokens_here)
    same = segment[:, None] == segment[None, :]
    logits = jnp.einsum("thd,shd->hts", queries, keys, preferred_element_type=jnp.float32)
    logits = jnp.where(same[None], logits, -1e30)
    top = jnp.max(logits, axis=-1, keepdims=True)
    expo = jnp.exp(logits - top)
    weights = (expo / jnp.sum(expo, axis=-1, keepdims=True)).astype(jnp.bfloat16)
    context = jnp.einsum("hts,shd->thd", weights, values, preferred_element_type=jnp.float32)
    context = context.astype(jnp.bfloat16).reshape(tokens_here, local_width)
    partial_value = jnp.dot(context, w_output, preferred_element_type=jnp.float32)
    attended = settle(partial_value, hidden, b_output, first_gain, first_shift, n_tensor)
    activated = jax.nn.gelu(
        jnp.dot(attended, w_up, preferred_element_type=jnp.float32) + b_up, approximate=False
    ).astype(jnp.bfloat16)
    partial_value = jnp.dot(activated, w_down, preferred_element_type=jnp.float32)
    states = settle(partial_value, attended, b_down, second_gain, second_shift, n_tensor)
    texts_here = lengths.shape[1]
    member = (segment[None, :] == jnp.arange(texts_here, dtype=jnp.int32)[:, None]).astype(
        jnp.bfloat16
    )
    pooled = (
        jnp.dot(member, states, preferred_element_type=jnp.float32)
        / lengths[0].astype(jnp.float32)[:, None]
    )
    unit = pooled * lax.rsqrt(jnp.sum(pooled * pooled, axis=-1, keepdims=True) + 1e-06)
    quarter = index.shape[1]
    unit_quarter = lax.dynamic_slice_in_dim(
        unit, lax.axis_index("tensor") * quarter, quarter, 1
    ).astype(jnp.bfloat16)
    row_base = lax.axis_index("dp") * index.shape[0]
    xor_ok = (
        is_power_of_two(n_dp)
        and is_power_of_two(n_tensor)
        and candidates.shape[0] % n_dp == 0
    )
    if xor_ok:
        gathered = all_gather_xor(unit_quarter, "dp", n_dp, levels_of(n_dp))
    else:
        gathered = lax.all_gather(unit_quarter, "dp", axis=0, tiled=True)
    all_texts = candidates.shape[0]
    shard_rows = index.shape[0]
    local_rows = candidates - row_base
    held = (local_rows >= 0) & (local_rows < shard_rows)
    tile = lax.dot_general(
        gathered, index, (((1,), (1,)), ((), ())), preferred_element_type=jnp.float32
    )
    wanted = jnp.clip(local_rows, 0, shard_rows - 1)
    minor = 128
    if shard_rows % minor == 0:
        major = shard_rows // minor
        major_hot = (
            (wanted // minor)[:, :, None] == jnp.arange(major, dtype=jnp.int32)[None, None, :]
        ).astype(jnp.float32)
        rows_of = jnp.einsum(
            "tca,tab->tcb",
            major_hot,
            tile.reshape(all_texts, major, minor),
            precision=lax.Precision.HIGH,
            preferred_element_type=jnp.float32,
        )
        minor_hot = (wanted % minor)[:, :, None] == jnp.arange(minor, dtype=jnp.int32)[None, None, :]
        picked = jnp.sum(jnp.where(minor_hot, rows_of, 0.0), axis=2)
    else:
        row_ids = jnp.arange(shard_rows, dtype=jnp.int32)
        chosen = wanted[:, :, None] == row_ids[None, None, :]
        picked = jnp.sum(jnp.where(chosen, tile[:, None, :], 0.0), axis=2)
    partial_scores = jnp.where(held, picked, 0.0)
    if not xor_ok:
        slice_scores = lax.psum_scatter(
            partial_scores, ("dp", "tensor"), scatter_dimension=0, tiled=True
        )
        scores = lax.all_gather(slice_scores, "tensor", axis=0, tiled=True)
        return (states, scores)
    text_scores, _ = reduce_scatter_xor(partial_scores, "dp", n_dp, levels_of(n_dp)[::-1])
    for k in levels_of(n_tensor):
        text_scores = text_scores + lax.ppermute(text_scores, "tensor", xor_pairs(n_tensor, k))
    return (states, text_scores)


def solution(mesh):
    placed = (
        P("dp", None),
        P("dp", None),
        P(None, None, "tensor"),
        P(None, "tensor"),
        P("tensor", None),
        P(),
        P(),
        P(),
        P(None, "tensor"),
        P("tensor"),
        P("tensor", None),
        P(),
        P(),
        P(),
        P("dp", "tensor"),
        P(),
    )
    n_dp = mesh.shape["dp"]
    n_tensor = mesh.shape["tensor"]

    def run(*args):
        return body(*args, n_dp=n_dp, n_tensor=n_tensor)

    return jax.shard_map(
        run, mesh=mesh, in_specs=placed, out_specs=(P("dp", None), P("dp", None)), check_vma=False
    )
```

```python
import math

import jax
import jax.numpy as jnp
from jax import lax
from jax.sharding import PartitionSpec as P

HEAD = 64


def layer_norm(values, gain, shift):
    centre = jnp.mean(values, axis=-1, keepdims=True)
    centred = values - centre
    spread = jnp.mean(centred * centred, axis=-1, keepdims=True)
    return centred * lax.rsqrt(spread + 1e-05) * gain + shift


def segment_of(pack_lengths, count):
    ends = jnp.cumsum(pack_lengths)
    position = jnp.arange(count, dtype=jnp.int32)
    return jnp.sum((position[:, None] >= ends[None, :]).astype(jnp.int32), axis=1)


def is_power_of_two(n):
    return n >= 1 and (n & (n - 1)) == 0


def xor_pairs(n, k):
    return [(i, i ^ k) for i in range(n)]


def levels_of(n):
    return [1 << j for j in range(int(math.log2(n)))] if n > 1 else []


def reduce_scatter_xor(value, axis, n, levels):
    index = lax.axis_index(axis)
    acc = value
    block = 0
    count = 1
    for k in levels:
        half = acc.shape[0] // 2
        bit = (index // k) % 2
        mine = lax.dynamic_slice_in_dim(acc, bit * half, half, 0)
        theirs = lax.dynamic_slice_in_dim(acc, (1 - bit) * half, half, 0)
        wire = jnp.float32 if value.dtype == jnp.float32 else jnp.bfloat16
        got = lax.ppermute(theirs.astype(wire), axis, xor_pairs(n, k))
        acc = mine.astype(jnp.float32) + got.astype(jnp.float32)
        count *= 2
        block = block * 2 + bit
    return acc, block


def all_gather_xor(value, axis, n, levels):
    index = lax.axis_index(axis)
    cur = value
    for k in levels:
        other = lax.ppermute(cur, axis, xor_pairs(n, k))
        bit = (index // k) % 2
        cur = jnp.where(bit == 0, jnp.concatenate([cur, other]), jnp.concatenate([other, cur]))
    return cur


def settle(partial_value, residual, bias, gain, shift, n_tensor):
    if n_tensor == 4 and partial_value.shape[0] % 2 == 0:
        return settle_by_chip(partial_value, residual, bias, gain, shift)
    if not is_power_of_two(n_tensor) or partial_value.shape[0] % n_tensor:
        total = lax.psum(partial_value.astype(jnp.bfloat16), "tensor").astype(jnp.float32)
        return layer_norm(total + bias + residual.astype(jnp.float32), gain, shift).astype(
            jnp.bfloat16
        )
    levels = levels_of(n_tensor)
    total, block = reduce_scatter_xor(partial_value.astype(jnp.bfloat16), "tensor", n_tensor, levels)
    rows = total.shape[0]
    own_residual = lax.dynamic_slice_in_dim(residual, block * rows, rows, 0)
    normed = layer_norm(total + bias + own_residual.astype(jnp.float32), gain, shift).astype(
        jnp.bfloat16
    )
    return all_gather_xor(normed, "tensor", n_tensor, levels[::-1])


def settle_by_chip(partial_value, residual, bias, gain, shift):
    index = lax.axis_index("tensor")
    low = index % 2
    half = partial_value.shape[0] // 2
    rounded = partial_value.astype(jnp.bfloat16)
    mine = lax.dynamic_slice_in_dim(rounded, low * half, half, 0)
    theirs = lax.dynamic_slice_in_dim(rounded, (1 - low) * half, half, 0)
    got = lax.ppermute(theirs, "tensor", xor_pairs(4, 1))
    chip_sum = (mine.astype(jnp.float32) + got.astype(jnp.float32)).astype(jnp.bfloat16)
    split = half // 2
    across = jnp.concatenate(
        [
            lax.ppermute(chip_sum[:split], "tensor", xor_pairs(4, 2)),
            lax.ppermute(chip_sum[split:], "tensor", xor_pairs(4, 2)),
        ]
    )
    total = chip_sum.astype(jnp.float32) + across.astype(jnp.float32)
    own_residual = lax.dynamic_slice_in_dim(residual, low * half, half, 0)
    normed = layer_norm(total + bias + own_residual.astype(jnp.float32), gain, shift).astype(
        jnp.bfloat16
    )
    other = lax.ppermute(normed, "tensor", xor_pairs(4, 1))
    return jnp.where(low == 0, jnp.concatenate([normed, other]), jnp.concatenate([other, normed]))


def body(
    hidden,
    lengths,
    w_qkv,
    b_qkv,
    w_output,
    b_output,
    first_gain,
    first_shift,
    w_up,
    b_up,
    w_down,
    b_down,
    second_gain,
    second_shift,
    index,
    candidates,
    n_dp,
    n_tensor,
):
    tokens_here = hidden.shape[0]
    local_width = w_qkv.shape[2]
    local_heads = local_width // HEAD
    projected = (
        jnp.einsum("td,jdf->jtf", hidden, w_qkv, preferred_element_type=jnp.float32)
        + b_qkv[:, None, :]
    )
    queries = (projected[0] * 0.125).astype(jnp.bfloat16).reshape(tokens_here, local_heads, HEAD)
    keys = projected[1].astype(jnp.bfloat16).reshape(tokens_here, local_heads, HEAD)
    values = projected[2].astype(jnp.bfloat16).reshape(tokens_here, local_heads, HEAD)
    segment = segment_of(lengths[0], tokens_here)
    same = segment[:, None] == segment[None, :]
    logits = jnp.einsum("thd,shd->hts", queries, keys, preferred_element_type=jnp.float32)
    logits = jnp.where(same[None], logits, -1e30)
    top = jnp.max(logits, axis=-1, keepdims=True)
    expo = jnp.exp(logits - top)
    weights = (expo / jnp.sum(expo, axis=-1, keepdims=True)).astype(jnp.bfloat16)
    context = jnp.einsum("hts,shd->thd", weights, values, preferred_element_type=jnp.float32)
    context = context.astype(jnp.bfloat16).reshape(tokens_here, local_width)
    partial_value = jnp.dot(context, w_output, preferred_element_type=jnp.float32)
    attended = settle(partial_value, hidden, b_output, first_gain, first_shift, n_tensor)
    activated = jax.nn.gelu(
        jnp.dot(attended, w_up, preferred_element_type=jnp.float32) + b_up, approximate=False
    ).astype(jnp.bfloat16)
    partial_value = jnp.dot(activated, w_down, preferred_element_type=jnp.float32)
    states = settle(partial_value, attended, b_down, second_gain, second_shift, n_tensor)
    texts_here = lengths.shape[1]
    member = (segment[None, :] == jnp.arange(texts_here, dtype=jnp.int32)[:, None]).astype(
        jnp.bfloat16
    )
    pooled = (
        jnp.dot(member, states, preferred_element_type=jnp.float32)
        / lengths[0].astype(jnp.float32)[:, None]
    )
    unit = pooled * lax.rsqrt(jnp.sum(pooled * pooled, axis=-1, keepdims=True) + 1e-06)
    quarter = index.shape[1]
    unit_quarter = lax.dynamic_slice_in_dim(
        unit, lax.axis_index("tensor") * quarter, quarter, 1
    ).astype(jnp.bfloat16)
    row_base = lax.axis_index("dp") * index.shape[0]
    xor_ok = (
        is_power_of_two(n_dp)
        and is_power_of_two(n_tensor)
        and candidates.shape[0] % n_dp == 0
    )
    if xor_ok:
        gathered = all_gather_xor(unit_quarter, "dp", n_dp, levels_of(n_dp))
    else:
        gathered = lax.all_gather(unit_quarter, "dp", axis=0, tiled=True)
    all_texts = candidates.shape[0]
    shard_rows = index.shape[0]
    local_rows = candidates - row_base
    held = (local_rows >= 0) & (local_rows < shard_rows)
    tile = lax.dot_general(
        gathered, index, (((1,), (1,)), ((), ())), preferred_element_type=jnp.float32
    )
    wanted = jnp.clip(local_rows, 0, shard_rows - 1)
    minor = 128
    if shard_rows % minor == 0:
        major = shard_rows // minor
        major_hot = (
            (wanted // minor)[:, :, None] == jnp.arange(major, dtype=jnp.int32)[None, None, :]
        ).astype(jnp.float32)
        rows_of = jnp.einsum(
            "tca,tab->tcb",
            major_hot,
            tile.reshape(all_texts, major, minor),
            precision=lax.Precision.HIGH,
            preferred_element_type=jnp.float32,
        )
        minor_hot = (wanted % minor)[:, :, None] == jnp.arange(minor, dtype=jnp.int32)[None, None, :]
        picked = jnp.sum(jnp.where(minor_hot, rows_of, 0.0), axis=2)
    else:
        row_ids = jnp.arange(shard_rows, dtype=jnp.int32)
        chosen = wanted[:, :, None] == row_ids[None, None, :]
        picked = jnp.sum(jnp.where(chosen, tile[:, None, :], 0.0), axis=2)
    partial_scores = jnp.where(held, picked, 0.0)
    if not xor_ok:
        slice_scores = lax.psum_scatter(
            partial_scores, ("dp", "tensor"), scatter_dimension=0, tiled=True
        )
        scores = lax.all_gather(slice_scores, "tensor", axis=0, tiled=True)
        return (states, scores)
    text_scores, _ = reduce_scatter_xor(partial_scores, "dp", n_dp, levels_of(n_dp)[::-1])
    for k in levels_of(n_tensor):
        text_scores = text_scores + lax.ppermute(text_scores, "tensor", xor_pairs(n_tensor, k))
    return (states, text_scores)


def solution(mesh):
    placed = (
        P("dp", None),
        P("dp", None),
        P(None, None, "tensor"),
        P(None, "tensor"),
        P("tensor", None),
        P(),
        P(),
        P(),
        P(None, "tensor"),
        P("tensor"),
        P("tensor", None),
        P(),
        P(),
        P(),
        P("dp", "tensor"),
        P(),
    )
    n_dp = mesh.shape["dp"]
    n_tensor = mesh.shape["tensor"]

    def run(*args):
        return body(*args, n_dp=n_dp, n_tensor=n_tensor)

    return jax.shard_map(
        run, mesh=mesh, in_specs=placed, out_specs=(P("dp", None), P("dp", None)), check_vma=False
    )
```

```python
import math

import jax
import jax.numpy as jnp
from jax import lax
from jax.sharding import PartitionSpec as P

HEAD = 64


def layer_norm(values, gain, shift):
    centre = jnp.mean(values, axis=-1, keepdims=True)
    centred = values - centre
    spread = jnp.mean(centred * centred, axis=-1, keepdims=True)
    return centred * lax.rsqrt(spread + 1e-05) * gain + shift


def segment_of(pack_lengths, count):
    ends = jnp.cumsum(pack_lengths)
    position = jnp.arange(count, dtype=jnp.int32)
    return jnp.sum((position[:, None] >= ends[None, :]).astype(jnp.int32), axis=1)


def is_power_of_two(n):
    return n >= 1 and (n & (n - 1)) == 0


def xor_pairs(n, k):
    return [(i, i ^ k) for i in range(n)]


def levels_of(n):
    return [1 << j for j in range(int(math.log2(n)))] if n > 1 else []


def reduce_scatter_xor(value, axis, n, levels):
    index = lax.axis_index(axis)
    acc = value
    block = 0
    count = 1
    for k in levels:
        half = acc.shape[0] // 2
        bit = (index // k) % 2
        mine = lax.dynamic_slice_in_dim(acc, bit * half, half, 0)
        theirs = lax.dynamic_slice_in_dim(acc, (1 - bit) * half, half, 0)
        wire = jnp.float32 if value.dtype == jnp.float32 else jnp.bfloat16
        got = lax.ppermute(theirs.astype(wire), axis, xor_pairs(n, k))
        acc = mine.astype(jnp.float32) + got.astype(jnp.float32)
        count *= 2
        block = block * 2 + bit
    return acc, block


def all_gather_xor(value, axis, n, levels):
    index = lax.axis_index(axis)
    cur = value
    for k in levels:
        other = lax.ppermute(cur, axis, xor_pairs(n, k))
        bit = (index // k) % 2
        cur = jnp.where(bit == 0, jnp.concatenate([cur, other]), jnp.concatenate([other, cur]))
    return cur


def settle(partial_value, residual, bias, gain, shift, n_tensor):
    if n_tensor == 4 and partial_value.shape[0] % 2 == 0:
        return settle_by_chip(partial_value, residual, bias, gain, shift)
    if not is_power_of_two(n_tensor) or partial_value.shape[0] % n_tensor:
        total = lax.psum(partial_value.astype(jnp.bfloat16), "tensor").astype(jnp.float32)
        return layer_norm(total + bias + residual.astype(jnp.float32), gain, shift).astype(
            jnp.bfloat16
        )
    levels = levels_of(n_tensor)
    total, block = reduce_scatter_xor(partial_value.astype(jnp.bfloat16), "tensor", n_tensor, levels)
    rows = total.shape[0]
    own_residual = lax.dynamic_slice_in_dim(residual, block * rows, rows, 0)
    normed = layer_norm(total + bias + own_residual.astype(jnp.float32), gain, shift).astype(
        jnp.bfloat16
    )
    return all_gather_xor(normed, "tensor", n_tensor, levels[::-1])


def settle_by_chip(partial_value, residual, bias, gain, shift):
    index = lax.axis_index("tensor")
    low = index % 2
    half = partial_value.shape[0] // 2
    rounded = partial_value.astype(jnp.bfloat16)
    mine = lax.dynamic_slice_in_dim(rounded, low * half, half, 0)
    theirs = lax.dynamic_slice_in_dim(rounded, (1 - low) * half, half, 0)
    got = lax.ppermute(theirs, "tensor", xor_pairs(4, 1))
    chip_sum = (mine.astype(jnp.float32) + got.astype(jnp.float32)).astype(jnp.bfloat16)
    across = lax.ppermute(chip_sum, "tensor", xor_pairs(4, 2))
    total = chip_sum.astype(jnp.float32) + across.astype(jnp.float32)
    own_residual = lax.dynamic_slice_in_dim(residual, low * half, half, 0)
    normed = layer_norm(total + bias + own_residual.astype(jnp.float32), gain, shift).astype(
        jnp.bfloat16
    )
    other = lax.ppermute(normed, "tensor", xor_pairs(4, 1))
    return jnp.where(low == 0, jnp.concatenate([normed, other]), jnp.concatenate([other, normed]))


def body(
    hidden,
    lengths,
    w_qkv,
    b_qkv,
    w_output,
    b_output,
    first_gain,
    first_shift,
    w_up,
    b_up,
    w_down,
    b_down,
    second_gain,
    second_shift,
    index,
    candidates,
    n_dp,
    n_tensor,
):
    tokens_here = hidden.shape[0]
    local_width = w_qkv.shape[2]
    local_heads = local_width // HEAD
    projected = (
        jnp.einsum("td,jdf->jtf", hidden, w_qkv, preferred_element_type=jnp.float32)
        + b_qkv[:, None, :]
    )
    queries = (projected[0] * 0.125).astype(jnp.bfloat16).reshape(tokens_here, local_heads, HEAD)
    keys = projected[1].astype(jnp.bfloat16).reshape(tokens_here, local_heads, HEAD)
    values = projected[2].astype(jnp.bfloat16).reshape(tokens_here, local_heads, HEAD)
    segment = segment_of(lengths[0], tokens_here)
    same = segment[:, None] == segment[None, :]
    logits = jnp.einsum("thd,shd->hts", queries, keys, preferred_element_type=jnp.float32)
    logits = jnp.where(same[None], logits, -1e30)
    top = jnp.max(logits, axis=-1, keepdims=True)
    expo = jnp.exp(logits - top)
    weights = (expo / jnp.sum(expo, axis=-1, keepdims=True)).astype(jnp.bfloat16)
    context = jnp.einsum("hts,shd->thd", weights, values, preferred_element_type=jnp.float32)
    context = context.astype(jnp.bfloat16).reshape(tokens_here, local_width)
    partial_value = jnp.dot(context, w_output, preferred_element_type=jnp.float32)
    attended = settle(partial_value, hidden, b_output, first_gain, first_shift, n_tensor)
    activated = jax.nn.gelu(
        jnp.dot(attended, w_up, preferred_element_type=jnp.float32) + b_up, approximate=False
    ).astype(jnp.bfloat16)
    partial_value = jnp.dot(activated, w_down, preferred_element_type=jnp.float32)
    states = settle(partial_value, attended, b_down, second_gain, second_shift, n_tensor)
    texts_here = lengths.shape[1]
    member = (segment[None, :] == jnp.arange(texts_here, dtype=jnp.int32)[:, None]).astype(
        jnp.bfloat16
    )
    pooled = (
        jnp.dot(member, states, preferred_element_type=jnp.float32)
        / lengths[0].astype(jnp.float32)[:, None]
    )
    unit = pooled * lax.rsqrt(jnp.sum(pooled * pooled, axis=-1, keepdims=True) + 1e-06)
    quarter = index.shape[1]
    unit_quarter = lax.dynamic_slice_in_dim(
        unit, lax.axis_index("tensor") * quarter, quarter, 1
    ).astype(jnp.bfloat16)
    row_base = lax.axis_index("dp") * index.shape[0]
    xor_ok = (
        is_power_of_two(n_dp)
        and is_power_of_two(n_tensor)
        and candidates.shape[0] % n_dp == 0
    )
    if xor_ok:
        gathered = all_gather_xor(unit_quarter, "dp", n_dp, levels_of(n_dp))
    else:
        gathered = lax.all_gather(unit_quarter, "dp", axis=0, tiled=True)
    all_texts = candidates.shape[0]
    shard_rows = index.shape[0]
    local_rows = candidates - row_base
    held = (local_rows >= 0) & (local_rows < shard_rows)

    def pick(packed):
        units_block, wanted = packed
        texts = units_block.shape[0]
        tile = lax.dot_general(
            units_block, index, (((1,), (1,)), ((), ())), preferred_element_type=jnp.float32
        )
        minor = 128
        if shard_rows % minor == 0:
            major = shard_rows // minor
            major_hot = (
                (wanted // minor)[:, :, None] == jnp.arange(major, dtype=jnp.int32)[None, None, :]
            ).astype(jnp.bfloat16)
            high = tile.astype(jnp.bfloat16)
            low = (tile - high.astype(jnp.float32)).astype(jnp.bfloat16)
            parts = jnp.concatenate(
                [high.reshape(texts, major, minor), low.reshape(texts, major, minor)], axis=2
            )
            chosen_parts = jnp.einsum(
                "tca,tab->tcb", major_hot, parts, preferred_element_type=jnp.float32
            )
            rows_of = chosen_parts[:, :, :minor] + chosen_parts[:, :, minor:]
            minor_hot = (wanted % minor)[:, :, None] == jnp.arange(minor, dtype=jnp.int32)[None, None, :]
            picked = jnp.sum(jnp.where(minor_hot, rows_of, 0.0), axis=2)
        else:
            row_ids = jnp.arange(shard_rows, dtype=jnp.int32)
            chosen = wanted[:, :, None] == row_ids[None, None, :]
            picked = jnp.sum(jnp.where(chosen, tile[:, None, :], 0.0), axis=2)
        return picked

    wanted_all = jnp.clip(local_rows, 0, shard_rows - 1)
    block_rows = math.gcd(all_texts, 128)
    if block_rows == all_texts:
        picked = pick((gathered, wanted_all))
    else:
        picked = lax.map(
            pick,
            (
                gathered.reshape(all_texts // block_rows, block_rows, -1),
                wanted_all.reshape(all_texts // block_rows, block_rows, -1),
            ),
        ).reshape(all_texts, -1)
    partial_scores = jnp.where(held, picked, 0.0)
    if not xor_ok:
        slice_scores = lax.psum_scatter(
            partial_scores, ("dp", "tensor"), scatter_dimension=0, tiled=True
        )
        scores = lax.all_gather(slice_scores, "tensor", axis=0, tiled=True)
        return (states, scores)
    text_scores, _ = reduce_scatter_xor(partial_scores, "dp", n_dp, levels_of(n_dp)[::-1])
    for k in levels_of(n_tensor):
        text_scores = text_scores + lax.ppermute(text_scores, "tensor", xor_pairs(n_tensor, k))
    return (states, text_scores)


def solution(mesh):
    placed = (
        P("dp", None),
        P("dp", None),
        P(None, None, "tensor"),
        P(None, "tensor"),
        P("tensor", None),
        P(),
        P(),
        P(),
        P(None, "tensor"),
        P("tensor"),
        P("tensor", None),
        P(),
        P(),
        P(),
        P("dp", "tensor"),
        P(),
    )
    n_dp = mesh.shape["dp"]
    n_tensor = mesh.shape["tensor"]

    def run(*args):
        return body(*args, n_dp=n_dp, n_tensor=n_tensor)

    return jax.shard_map(
        run, mesh=mesh, in_specs=placed, out_specs=(P("dp", None), P("dp", None)), check_vma=False
    )
```

```python
import math

import jax
import jax.numpy as jnp
from jax import lax
from jax.sharding import PartitionSpec as P

HEAD = 64


def layer_norm(values, gain, shift):
    centre = jnp.mean(values, axis=-1, keepdims=True)
    centred = values - centre
    spread = jnp.mean(centred * centred, axis=-1, keepdims=True)
    return centred * lax.rsqrt(spread + 1e-05) * gain + shift


def segment_of(pack_lengths, count):
    ends = jnp.cumsum(pack_lengths)
    position = jnp.arange(count, dtype=jnp.int32)
    return jnp.sum((position[:, None] >= ends[None, :]).astype(jnp.int32), axis=1)


def is_power_of_two(n):
    return n >= 1 and (n & (n - 1)) == 0


def xor_pairs(n, k):
    return [(i, i ^ k) for i in range(n)]


def levels_of(n):
    return [1 << j for j in range(int(math.log2(n)))] if n > 1 else []


def reduce_scatter_xor(value, axis, n, levels):
    index = lax.axis_index(axis)
    acc = value
    block = 0
    count = 1
    for k in levels:
        half = acc.shape[0] // 2
        bit = (index // k) % 2
        mine = lax.dynamic_slice_in_dim(acc, bit * half, half, 0)
        theirs = lax.dynamic_slice_in_dim(acc, (1 - bit) * half, half, 0)
        wire = jnp.float32 if value.dtype == jnp.float32 else jnp.bfloat16
        got = lax.ppermute(theirs.astype(wire), axis, xor_pairs(n, k))
        acc = mine.astype(jnp.float32) + got.astype(jnp.float32)
        count *= 2
        block = block * 2 + bit
    return acc, block


def all_gather_xor(value, axis, n, levels):
    index = lax.axis_index(axis)
    cur = value
    for k in levels:
        other = lax.ppermute(cur, axis, xor_pairs(n, k))
        bit = (index // k) % 2
        cur = jnp.where(bit == 0, jnp.concatenate([cur, other]), jnp.concatenate([other, cur]))
    return cur


def settle(partial_value, residual, bias, gain, shift, n_tensor):
    if n_tensor == 4 and partial_value.shape[0] % 2 == 0:
        return settle_by_chip(partial_value, residual, bias, gain, shift)
    if not is_power_of_two(n_tensor) or partial_value.shape[0] % n_tensor:
        total = lax.psum(partial_value.astype(jnp.bfloat16), "tensor").astype(jnp.float32)
        return layer_norm(total + bias + residual.astype(jnp.float32), gain, shift).astype(
            jnp.bfloat16
        )
    levels = levels_of(n_tensor)
    total, block = reduce_scatter_xor(partial_value.astype(jnp.bfloat16), "tensor", n_tensor, levels)
    rows = total.shape[0]
    own_residual = lax.dynamic_slice_in_dim(residual, block * rows, rows, 0)
    normed = layer_norm(total + bias + own_residual.astype(jnp.float32), gain, shift).astype(
        jnp.bfloat16
    )
    return all_gather_xor(normed, "tensor", n_tensor, levels[::-1])


def settle_by_chip(partial_value, residual, bias, gain, shift):
    index = lax.axis_index("tensor")
    low = index % 2
    half = partial_value.shape[0] // 2
    rounded = partial_value.astype(jnp.bfloat16)
    mine = lax.dynamic_slice_in_dim(rounded, low * half, half, 0)
    theirs = lax.dynamic_slice_in_dim(rounded, (1 - low) * half, half, 0)
    got = lax.ppermute(theirs, "tensor", xor_pairs(4, 1))
    chip_sum = (mine.astype(jnp.float32) + got.astype(jnp.float32)).astype(jnp.bfloat16)
    across = lax.ppermute(chip_sum, "tensor", xor_pairs(4, 2))
    total = chip_sum.astype(jnp.float32) + across.astype(jnp.float32)
    own_residual = lax.dynamic_slice_in_dim(residual, low * half, half, 0)
    normed = layer_norm(total + bias + own_residual.astype(jnp.float32), gain, shift).astype(
        jnp.bfloat16
    )
    other = lax.ppermute(normed, "tensor", xor_pairs(4, 1))
    return jnp.where(low == 0, jnp.concatenate([normed, other]), jnp.concatenate([other, normed]))


def body(
    hidden,
    lengths,
    w_qkv,
    b_qkv,
    w_output,
    b_output,
    first_gain,
    first_shift,
    w_up,
    b_up,
    w_down,
    b_down,
    second_gain,
    second_shift,
    index,
    candidates,
    n_dp,
    n_tensor,
):
    tokens_here = hidden.shape[0]
    local_width = w_qkv.shape[2]
    local_heads = local_width // HEAD
    projected = (
        jnp.einsum("td,jdf->jtf", hidden, w_qkv, preferred_element_type=jnp.float32)
        + b_qkv[:, None, :]
    )
    queries = (projected[0] * 0.125).astype(jnp.bfloat16).reshape(tokens_here, local_heads, HEAD)
    keys = projected[1].astype(jnp.bfloat16).reshape(tokens_here, local_heads, HEAD)
    values = projected[2].astype(jnp.bfloat16).reshape(tokens_here, local_heads, HEAD)
    segment = segment_of(lengths[0], tokens_here)
    same = segment[:, None] == segment[None, :]
    logits = jnp.einsum("thd,shd->hts", queries, keys, preferred_element_type=jnp.float32)
    logits = jnp.where(same[None], logits, -1e30)
    top = jnp.max(logits, axis=-1, keepdims=True)
    expo = jnp.exp(logits - top)
    weights = (expo / jnp.sum(expo, axis=-1, keepdims=True)).astype(jnp.bfloat16)
    context = jnp.einsum("hts,shd->thd", weights, values, preferred_element_type=jnp.float32)
    context = context.astype(jnp.bfloat16).reshape(tokens_here, local_width)
    partial_value = jnp.dot(context, w_output, preferred_element_type=jnp.float32)
    attended = settle(partial_value, hidden, b_output, first_gain, first_shift, n_tensor)
    activated = jax.nn.gelu(
        jnp.dot(attended, w_up, preferred_element_type=jnp.float32) + b_up, approximate=False
    ).astype(jnp.bfloat16)
    partial_value = jnp.dot(activated, w_down, preferred_element_type=jnp.float32)
    states = settle(partial_value, attended, b_down, second_gain, second_shift, n_tensor)
    texts_here = lengths.shape[1]
    member = (segment[None, :] == jnp.arange(texts_here, dtype=jnp.int32)[:, None]).astype(
        jnp.bfloat16
    )
    pooled = (
        jnp.dot(member, states, preferred_element_type=jnp.float32)
        / lengths[0].astype(jnp.float32)[:, None]
    )
    unit = pooled * lax.rsqrt(jnp.sum(pooled * pooled, axis=-1, keepdims=True) + 1e-06)
    quarter = index.shape[1]
    unit_quarter = lax.dynamic_slice_in_dim(
        unit, lax.axis_index("tensor") * quarter, quarter, 1
    ).astype(jnp.bfloat16)
    row_base = lax.axis_index("dp") * index.shape[0]
    xor_ok = (
        is_power_of_two(n_dp)
        and is_power_of_two(n_tensor)
        and candidates.shape[0] % n_dp == 0
    )
    all_texts = candidates.shape[0]
    shard_rows = index.shape[0]
    local_rows = candidates - row_base
    held = (local_rows >= 0) & (local_rows < shard_rows)

    def pick(packed):
        units_block, wanted = packed
        texts = units_block.shape[0]
        tile = lax.dot_general(
            units_block, index, (((1,), (1,)), ((), ())), preferred_element_type=jnp.float32
        )
        minor = 128
        if shard_rows % minor == 0:
            major = shard_rows // minor
            major_hot = (
                (wanted // minor)[:, :, None] == jnp.arange(major, dtype=jnp.int32)[None, None, :]
            ).astype(jnp.bfloat16)
            high = tile.astype(jnp.bfloat16)
            low = (tile - high.astype(jnp.float32)).astype(jnp.bfloat16)
            parts = jnp.concatenate(
                [high.reshape(texts, major, minor), low.reshape(texts, major, minor)], axis=2
            )
            chosen_parts = jnp.einsum(
                "tca,tab->tcb", major_hot, parts, preferred_element_type=jnp.float32
            )
            rows_of = chosen_parts[:, :, :minor] + chosen_parts[:, :, minor:]
            minor_hot = (wanted % minor)[:, :, None] == jnp.arange(minor, dtype=jnp.int32)[None, None, :]
            picked = jnp.sum(jnp.where(minor_hot, rows_of, 0.0), axis=2)
        else:
            row_ids = jnp.arange(shard_rows, dtype=jnp.int32)
            chosen = wanted[:, :, None] == row_ids[None, None, :]
            picked = jnp.sum(jnp.where(chosen, tile[:, None, :], 0.0), axis=2)
        return picked

    wanted_all = jnp.clip(local_rows, 0, shard_rows - 1)

    def pick_all(units_rows, wanted, keep):
        texts = units_rows.shape[0]
        block_rows = math.gcd(texts, 128)
        if block_rows == texts:
            picked = pick((units_rows, wanted))
        else:
            picked = lax.map(
                pick,
                (
                    units_rows.reshape(texts // block_rows, block_rows, -1),
                    wanted.reshape(texts // block_rows, block_rows, -1),
                ),
            ).reshape(texts, -1)
        return jnp.where(keep, picked, 0.0)

    if not xor_ok or n_dp < 2:
        gathered = lax.all_gather(unit_quarter, "dp", axis=0, tiled=True)
        partial_scores = pick_all(gathered, wanted_all, held)
        slice_scores = lax.psum_scatter(
            partial_scores, ("dp", "tensor"), scatter_dimension=0, tiled=True
        )
        scores = lax.all_gather(slice_scores, "tensor", axis=0, tiled=True)
        return (states, scores)
    levels = levels_of(n_dp)
    last = levels[-1]
    near = all_gather_xor(unit_quarter, "dp", n_dp, levels[:-1])
    far = lax.ppermute(near, "dp", xor_pairs(n_dp, last))
    top = (lax.axis_index("dp") // last) % 2
    half = all_texts // 2
    near_scores = pick_all(
        near,
        lax.dynamic_slice_in_dim(wanted_all, top * half, half, 0),
        lax.dynamic_slice_in_dim(held, top * half, half, 0),
    )
    far_scores = pick_all(
        far,
        lax.dynamic_slice_in_dim(wanted_all, (1 - top) * half, half, 0),
        lax.dynamic_slice_in_dim(held, (1 - top) * half, half, 0),
    )
    kept = near_scores + lax.ppermute(far_scores, "dp", xor_pairs(n_dp, last))
    text_scores, _ = reduce_scatter_xor(kept, "dp", n_dp, levels[:-1][::-1])
    for k in levels_of(n_tensor):
        text_scores = text_scores + lax.ppermute(text_scores, "tensor", xor_pairs(n_tensor, k))
    return (states, text_scores)


def solution(mesh):
    placed = (
        P("dp", None),
        P("dp", None),
        P(None, None, "tensor"),
        P(None, "tensor"),
        P("tensor", None),
        P(),
        P(),
        P(),
        P(None, "tensor"),
        P("tensor"),
        P("tensor", None),
        P(),
        P(),
        P(),
        P("dp", "tensor"),
        P(),
    )
    n_dp = mesh.shape["dp"]
    n_tensor = mesh.shape["tensor"]

    def run(*args):
        return body(*args, n_dp=n_dp, n_tensor=n_tensor)

    return jax.shard_map(
        run, mesh=mesh, in_specs=placed, out_specs=(P("dp", None), P("dp", None)), check_vma=False
    )
```

```python
import math

import jax
import jax.numpy as jnp
from jax import lax
from jax.sharding import PartitionSpec as P

HEAD = 64


def layer_norm(values, gain, shift):
    centre = jnp.mean(values, axis=-1, keepdims=True)
    centred = values - centre
    spread = jnp.mean(centred * centred, axis=-1, keepdims=True)
    return centred * lax.rsqrt(spread + 1e-05) * gain + shift


def segment_of(pack_lengths, count):
    ends = jnp.cumsum(pack_lengths)
    position = jnp.arange(count, dtype=jnp.int32)
    return jnp.sum((position[:, None] >= ends[None, :]).astype(jnp.int32), axis=1)


def is_power_of_two(n):
    return n >= 1 and (n & (n - 1)) == 0


def xor_pairs(n, k):
    return [(i, i ^ k) for i in range(n)]


def levels_of(n):
    return [1 << j for j in range(int(math.log2(n)))] if n > 1 else []


def reduce_scatter_xor(value, axis, n, levels):
    index = lax.axis_index(axis)
    acc = value
    block = 0
    count = 1
    for k in levels:
        half = acc.shape[0] // 2
        bit = (index // k) % 2
        mine = lax.dynamic_slice_in_dim(acc, bit * half, half, 0)
        theirs = lax.dynamic_slice_in_dim(acc, (1 - bit) * half, half, 0)
        wire = jnp.float32 if value.dtype == jnp.float32 else jnp.bfloat16
        got = lax.ppermute(theirs.astype(wire), axis, xor_pairs(n, k))
        acc = mine.astype(jnp.float32) + got.astype(jnp.float32)
        count *= 2
        block = block * 2 + bit
    return acc, block


def all_gather_xor(value, axis, n, levels):
    index = lax.axis_index(axis)
    cur = value
    for k in levels:
        other = lax.ppermute(cur, axis, xor_pairs(n, k))
        bit = (index // k) % 2
        cur = jnp.where(bit == 0, jnp.concatenate([cur, other]), jnp.concatenate([other, cur]))
    return cur


def settle(partial_value, residual, bias, gain, shift, n_tensor):
    if n_tensor == 4 and partial_value.shape[0] % 2 == 0:
        return settle_by_chip(partial_value, residual, bias, gain, shift)
    if not is_power_of_two(n_tensor) or partial_value.shape[0] % n_tensor:
        total = lax.psum(partial_value.astype(jnp.bfloat16), "tensor").astype(jnp.float32)
        return layer_norm(total + bias + residual.astype(jnp.float32), gain, shift).astype(
            jnp.bfloat16
        )
    levels = levels_of(n_tensor)
    total, block = reduce_scatter_xor(partial_value.astype(jnp.bfloat16), "tensor", n_tensor, levels)
    rows = total.shape[0]
    own_residual = lax.dynamic_slice_in_dim(residual, block * rows, rows, 0)
    normed = layer_norm(total + bias + own_residual.astype(jnp.float32), gain, shift).astype(
        jnp.bfloat16
    )
    return all_gather_xor(normed, "tensor", n_tensor, levels[::-1])


def settle_by_chip(partial_value, residual, bias, gain, shift):
    index = lax.axis_index("tensor")
    low = index % 2
    if callable(partial_value):
        half = residual.shape[0] // 2
        theirs = partial_value((1 - low) * half, half).astype(jnp.bfloat16)
        got = lax.ppermute(theirs, "tensor", xor_pairs(4, 1))
        mine = partial_value(low * half, half).astype(jnp.bfloat16)
    else:
        half = partial_value.shape[0] // 2
        rounded = partial_value.astype(jnp.bfloat16)
        mine = lax.dynamic_slice_in_dim(rounded, low * half, half, 0)
        theirs = lax.dynamic_slice_in_dim(rounded, (1 - low) * half, half, 0)
        got = lax.ppermute(theirs, "tensor", xor_pairs(4, 1))
    chip_sum = (mine.astype(jnp.float32) + got.astype(jnp.float32)).astype(jnp.bfloat16)
    across = lax.ppermute(chip_sum, "tensor", xor_pairs(4, 2))
    total = chip_sum.astype(jnp.float32) + across.astype(jnp.float32)
    own_residual = lax.dynamic_slice_in_dim(residual, low * half, half, 0)
    normed = layer_norm(total + bias + own_residual.astype(jnp.float32), gain, shift).astype(
        jnp.bfloat16
    )
    other = lax.ppermute(normed, "tensor", xor_pairs(4, 1))
    return jnp.where(low == 0, jnp.concatenate([normed, other]), jnp.concatenate([other, normed]))


def body(
    hidden,
    lengths,
    w_qkv,
    b_qkv,
    w_output,
    b_output,
    first_gain,
    first_shift,
    w_up,
    b_up,
    w_down,
    b_down,
    second_gain,
    second_shift,
    index,
    candidates,
    n_dp,
    n_tensor,
):
    tokens_here = hidden.shape[0]
    local_width = w_qkv.shape[2]
    local_heads = local_width // HEAD
    projected = (
        jnp.einsum("td,jdf->jtf", hidden, w_qkv, preferred_element_type=jnp.float32)
        + b_qkv[:, None, :]
    )
    queries = (projected[0] * 0.125).astype(jnp.bfloat16).reshape(tokens_here, local_heads, HEAD)
    keys = projected[1].astype(jnp.bfloat16).reshape(tokens_here, local_heads, HEAD)
    values = projected[2].astype(jnp.bfloat16).reshape(tokens_here, local_heads, HEAD)
    segment = segment_of(lengths[0], tokens_here)
    same = segment[:, None] == segment[None, :]
    logits = jnp.einsum("thd,shd->hts", queries, keys, preferred_element_type=jnp.float32)
    logits = jnp.where(same[None], logits, -1e30)
    top = jnp.max(logits, axis=-1, keepdims=True)
    expo = jnp.exp(logits - top)
    weights = (expo / jnp.sum(expo, axis=-1, keepdims=True)).astype(jnp.bfloat16)
    context = jnp.einsum("hts,shd->thd", weights, values, preferred_element_type=jnp.float32)
    context = context.astype(jnp.bfloat16).reshape(tokens_here, local_width)
    if n_tensor == 4 and tokens_here % 2 == 0:

        def projected_rows(start, count):
            rows = lax.dynamic_slice_in_dim(context, start, count, 0)
            return jnp.dot(rows, w_output, preferred_element_type=jnp.float32)

        attended = settle_by_chip(projected_rows, hidden, b_output, first_gain, first_shift)
    else:
        partial_value = jnp.dot(context, w_output, preferred_element_type=jnp.float32)
        attended = settle(partial_value, hidden, b_output, first_gain, first_shift, n_tensor)
    activated = jax.nn.gelu(
        jnp.dot(attended, w_up, preferred_element_type=jnp.float32) + b_up, approximate=False
    ).astype(jnp.bfloat16)
    partial_value = jnp.dot(activated, w_down, preferred_element_type=jnp.float32)
    states = settle(partial_value, attended, b_down, second_gain, second_shift, n_tensor)
    texts_here = lengths.shape[1]
    member = (segment[None, :] == jnp.arange(texts_here, dtype=jnp.int32)[:, None]).astype(
        jnp.bfloat16
    )
    pooled = (
        jnp.dot(member, states, preferred_element_type=jnp.float32)
        / lengths[0].astype(jnp.float32)[:, None]
    )
    unit = pooled * lax.rsqrt(jnp.sum(pooled * pooled, axis=-1, keepdims=True) + 1e-06)
    quarter = index.shape[1]
    unit_quarter = lax.dynamic_slice_in_dim(
        unit, lax.axis_index("tensor") * quarter, quarter, 1
    ).astype(jnp.bfloat16)
    row_base = lax.axis_index("dp") * index.shape[0]
    xor_ok = (
        is_power_of_two(n_dp)
        and is_power_of_two(n_tensor)
        and candidates.shape[0] % n_dp == 0
    )
    if xor_ok:
        gathered = all_gather_xor(unit_quarter, "dp", n_dp, levels_of(n_dp))
    else:
        gathered = lax.all_gather(unit_quarter, "dp", axis=0, tiled=True)
    all_texts = candidates.shape[0]
    shard_rows = index.shape[0]
    local_rows = candidates - row_base
    held = (local_rows >= 0) & (local_rows < shard_rows)

    def pick(packed):
        units_block, wanted = packed
        texts = units_block.shape[0]
        tile = lax.dot_general(
            units_block, index, (((1,), (1,)), ((), ())), preferred_element_type=jnp.float32
        )
        minor = 128
        if shard_rows % minor == 0:
            major = shard_rows // minor
            major_hot = (
                (wanted // minor)[:, :, None] == jnp.arange(major, dtype=jnp.int32)[None, None, :]
            ).astype(jnp.bfloat16)
            high = tile.astype(jnp.bfloat16)
            low = (tile - high.astype(jnp.float32)).astype(jnp.bfloat16)
            parts = jnp.concatenate(
                [high.reshape(texts, major, minor), low.reshape(texts, major, minor)], axis=2
            )
            chosen_parts = jnp.einsum(
                "tca,tab->tcb", major_hot, parts, preferred_element_type=jnp.float32
            )
            rows_of = chosen_parts[:, :, :minor] + chosen_parts[:, :, minor:]
            minor_hot = (wanted % minor)[:, :, None] == jnp.arange(minor, dtype=jnp.int32)[None, None, :]
            picked = jnp.sum(jnp.where(minor_hot, rows_of, 0.0), axis=2)
        else:
            row_ids = jnp.arange(shard_rows, dtype=jnp.int32)
            chosen = wanted[:, :, None] == row_ids[None, None, :]
            picked = jnp.sum(jnp.where(chosen, tile[:, None, :], 0.0), axis=2)
        return picked

    wanted_all = jnp.clip(local_rows, 0, shard_rows - 1)
    block_rows = math.gcd(all_texts, 128)
    if block_rows == all_texts:
        picked = pick((gathered, wanted_all))
    else:
        picked = lax.map(
            pick,
            (
                gathered.reshape(all_texts // block_rows, block_rows, -1),
                wanted_all.reshape(all_texts // block_rows, block_rows, -1),
            ),
        ).reshape(all_texts, -1)
    partial_scores = jnp.where(held, picked, 0.0)
    if not xor_ok:
        slice_scores = lax.psum_scatter(
            partial_scores, ("dp", "tensor"), scatter_dimension=0, tiled=True
        )
        scores = lax.all_gather(slice_scores, "tensor", axis=0, tiled=True)
        return (states, scores)
    text_scores, _ = reduce_scatter_xor(partial_scores, "dp", n_dp, levels_of(n_dp)[::-1])
    for k in levels_of(n_tensor):
        text_scores = text_scores + lax.ppermute(text_scores, "tensor", xor_pairs(n_tensor, k))
    return (states, text_scores)


def solution(mesh):
    placed = (
        P("dp", None),
        P("dp", None),
        P(None, None, "tensor"),
        P(None, "tensor"),
        P("tensor", None),
        P(),
        P(),
        P(),
        P(None, "tensor"),
        P("tensor"),
        P("tensor", None),
        P(),
        P(),
        P(),
        P("dp", "tensor"),
        P(),
    )
    n_dp = mesh.shape["dp"]
    n_tensor = mesh.shape["tensor"]

    def run(*args):
        return body(*args, n_dp=n_dp, n_tensor=n_tensor)

    return jax.shard_map(
        run, mesh=mesh, in_specs=placed, out_specs=(P("dp", None), P("dp", None)), check_vma=False
    )
```

```python
import math

import jax
import jax.numpy as jnp
from jax import lax
from jax.sharding import PartitionSpec as P

HEAD = 64


def layer_norm(values, gain, shift):
    centre = jnp.mean(values, axis=-1, keepdims=True)
    centred = values - centre
    spread = jnp.mean(centred * centred, axis=-1, keepdims=True)
    return centred * lax.rsqrt(spread + 1e-05) * gain + shift


def segment_of(pack_lengths, count):
    ends = jnp.cumsum(pack_lengths)
    position = jnp.arange(count, dtype=jnp.int32)
    return jnp.sum((position[:, None] >= ends[None, :]).astype(jnp.int32), axis=1)


def is_power_of_two(n):
    return n >= 1 and (n & (n - 1)) == 0


def xor_pairs(n, k):
    return [(i, i ^ k) for i in range(n)]


def levels_of(n):
    return [1 << j for j in range(int(math.log2(n)))] if n > 1 else []


def reduce_scatter_xor(value, axis, n, levels):
    index = lax.axis_index(axis)
    acc = value
    block = 0
    count = 1
    for k in levels:
        half = acc.shape[0] // 2
        bit = (index // k) % 2
        mine = lax.dynamic_slice_in_dim(acc, bit * half, half, 0)
        theirs = lax.dynamic_slice_in_dim(acc, (1 - bit) * half, half, 0)
        wire = jnp.float32 if value.dtype == jnp.float32 else jnp.bfloat16
        got = lax.ppermute(theirs.astype(wire), axis, xor_pairs(n, k))
        acc = mine.astype(jnp.float32) + got.astype(jnp.float32)
        count *= 2
        block = block * 2 + bit
    return acc, block


def all_gather_xor(value, axis, n, levels):
    index = lax.axis_index(axis)
    cur = value
    for k in levels:
        other = lax.ppermute(cur, axis, xor_pairs(n, k))
        bit = (index // k) % 2
        cur = jnp.where(bit == 0, jnp.concatenate([cur, other]), jnp.concatenate([other, cur]))
    return cur


def settle(partial_value, residual, bias, gain, shift, n_tensor):
    if n_tensor == 4 and partial_value.shape[0] % 2 == 0:
        return settle_by_chip(partial_value, residual, bias, gain, shift)
    if not is_power_of_two(n_tensor) or partial_value.shape[0] % n_tensor:
        total = lax.psum(partial_value.astype(jnp.bfloat16), "tensor").astype(jnp.float32)
        return layer_norm(total + bias + residual.astype(jnp.float32), gain, shift).astype(
            jnp.bfloat16
        )
    levels = levels_of(n_tensor)
    total, block = reduce_scatter_xor(partial_value.astype(jnp.bfloat16), "tensor", n_tensor, levels)
    rows = total.shape[0]
    own_residual = lax.dynamic_slice_in_dim(residual, block * rows, rows, 0)
    normed = layer_norm(total + bias + own_residual.astype(jnp.float32), gain, shift).astype(
        jnp.bfloat16
    )
    return all_gather_xor(normed, "tensor", n_tensor, levels[::-1])


def settle_by_chip(partial_value, residual, bias, gain, shift):
    index = lax.axis_index("tensor")
    low = index % 2
    half = partial_value.shape[0] // 2
    rounded = partial_value.astype(jnp.bfloat16)
    mine = lax.dynamic_slice_in_dim(rounded, low * half, half, 0)
    theirs = lax.dynamic_slice_in_dim(rounded, (1 - low) * half, half, 0)
    got = lax.ppermute(theirs, "tensor", xor_pairs(4, 1))
    chip_sum = (mine.astype(jnp.float32) + got.astype(jnp.float32)).astype(jnp.bfloat16)
    across = lax.ppermute(chip_sum, "tensor", xor_pairs(4, 2))
    total = chip_sum.astype(jnp.float32) + across.astype(jnp.float32)
    own_residual = lax.dynamic_slice_in_dim(residual, low * half, half, 0)
    normed = layer_norm(total + bias + own_residual.astype(jnp.float32), gain, shift).astype(
        jnp.bfloat16
    )
    other = lax.ppermute(normed, "tensor", xor_pairs(4, 1))
    return jnp.where(low == 0, jnp.concatenate([normed, other]), jnp.concatenate([other, normed]))


def body(
    hidden,
    lengths,
    w_qkv,
    b_qkv,
    w_output,
    b_output,
    first_gain,
    first_shift,
    w_up,
    b_up,
    w_down,
    b_down,
    second_gain,
    second_shift,
    index,
    candidates,
    n_dp,
    n_tensor,
):
    tokens_here = hidden.shape[0]
    local_width = w_qkv.shape[2]
    local_heads = local_width // HEAD
    scale = jnp.array([0.125, 1.0, 1.0], jnp.float32)[:, None, None]
    projected = (
        (
            jnp.einsum("td,jdf->jtf", hidden, w_qkv, preferred_element_type=jnp.float32)
            + b_qkv[:, None, :]
        )
        * scale
    ).astype(jnp.bfloat16)
    queries = projected[0].reshape(tokens_here, local_heads, HEAD)
    keys = projected[1].reshape(tokens_here, local_heads, HEAD)
    values = projected[2].reshape(tokens_here, local_heads, HEAD)
    segment = segment_of(lengths[0], tokens_here)
    same = segment[:, None] == segment[None, :]
    logits = jnp.einsum("thd,shd->hts", queries, keys, preferred_element_type=jnp.float32)
    logits = jnp.where(same[None], logits, -1e30)
    top = jnp.max(logits, axis=-1, keepdims=True)
    expo = jnp.exp(logits - top)
    weights = (expo / jnp.sum(expo, axis=-1, keepdims=True)).astype(jnp.bfloat16)
    context = jnp.einsum("hts,shd->thd", weights, values, preferred_element_type=jnp.float32)
    context = context.astype(jnp.bfloat16).reshape(tokens_here, local_width)
    partial_value = jnp.dot(context, w_output, preferred_element_type=jnp.float32)
    attended = settle(partial_value, hidden, b_output, first_gain, first_shift, n_tensor)
    activated = jax.nn.gelu(
        jnp.dot(attended, w_up, preferred_element_type=jnp.float32) + b_up, approximate=False
    ).astype(jnp.bfloat16)
    partial_value = jnp.dot(activated, w_down, preferred_element_type=jnp.float32)
    states = settle(partial_value, attended, b_down, second_gain, second_shift, n_tensor)
    texts_here = lengths.shape[1]
    member = (segment[None, :] == jnp.arange(texts_here, dtype=jnp.int32)[:, None]).astype(
        jnp.bfloat16
    )
    pooled = (
        jnp.dot(member, states, preferred_element_type=jnp.float32)
        / lengths[0].astype(jnp.float32)[:, None]
    )
    unit = pooled * lax.rsqrt(jnp.sum(pooled * pooled, axis=-1, keepdims=True) + 1e-06)
    quarter = index.shape[1]
    unit_quarter = lax.dynamic_slice_in_dim(
        unit, lax.axis_index("tensor") * quarter, quarter, 1
    ).astype(jnp.bfloat16)
    row_base = lax.axis_index("dp") * index.shape[0]
    xor_ok = (
        is_power_of_two(n_dp)
        and is_power_of_two(n_tensor)
        and candidates.shape[0] % n_dp == 0
    )
    if xor_ok:
        gathered = all_gather_xor(unit_quarter, "dp", n_dp, levels_of(n_dp))
    else:
        gathered = lax.all_gather(unit_quarter, "dp", axis=0, tiled=True)
    all_texts = candidates.shape[0]
    shard_rows = index.shape[0]
    local_rows = candidates - row_base
    held = (local_rows >= 0) & (local_rows < shard_rows)

    def pick(packed):
        units_block, wanted = packed
        texts = units_block.shape[0]
        tile = lax.dot_general(
            units_block, index, (((1,), (1,)), ((), ())), preferred_element_type=jnp.float32
        )
        minor = 128
        if shard_rows % minor == 0:
            major = shard_rows // minor
            major_hot = (
                (wanted // minor)[:, :, None] == jnp.arange(major, dtype=jnp.int32)[None, None, :]
            ).astype(jnp.bfloat16)
            high = tile.astype(jnp.bfloat16)
            low = (tile - high.astype(jnp.float32)).astype(jnp.bfloat16)
            parts = jnp.concatenate(
                [high.reshape(texts, major, minor), low.reshape(texts, major, minor)], axis=2
            )
            chosen_parts = jnp.einsum(
                "tca,tab->tcb", major_hot, parts, preferred_element_type=jnp.float32
            )
            rows_of = chosen_parts[:, :, :minor] + chosen_parts[:, :, minor:]
            minor_hot = (wanted % minor)[:, :, None] == jnp.arange(minor, dtype=jnp.int32)[None, None, :]
            picked = jnp.sum(jnp.where(minor_hot, rows_of, 0.0), axis=2)
        else:
            row_ids = jnp.arange(shard_rows, dtype=jnp.int32)
            chosen = wanted[:, :, None] == row_ids[None, None, :]
            picked = jnp.sum(jnp.where(chosen, tile[:, None, :], 0.0), axis=2)
        return picked

    wanted_all = jnp.clip(local_rows, 0, shard_rows - 1)
    block_rows = math.gcd(all_texts, 128)
    if block_rows == all_texts:
        picked = pick((gathered, wanted_all))
    else:
        picked = lax.map(
            pick,
            (
                gathered.reshape(all_texts // block_rows, block_rows, -1),
                wanted_all.reshape(all_texts // block_rows, block_rows, -1),
            ),
        ).reshape(all_texts, -1)
    partial_scores = jnp.where(held, picked, 0.0)
    if not xor_ok:
        slice_scores = lax.psum_scatter(
            partial_scores, ("dp", "tensor"), scatter_dimension=0, tiled=True
        )
        scores = lax.all_gather(slice_scores, "tensor", axis=0, tiled=True)
        return (states, scores)
    text_scores, _ = reduce_scatter_xor(partial_scores, "dp", n_dp, levels_of(n_dp)[::-1])
    for k in levels_of(n_tensor):
        text_scores = text_scores + lax.ppermute(text_scores, "tensor", xor_pairs(n_tensor, k))
    return (states, text_scores)


def solution(mesh):
    placed = (
        P("dp", None),
        P("dp", None),
        P(None, None, "tensor"),
        P(None, "tensor"),
        P("tensor", None),
        P(),
        P(),
        P(),
        P(None, "tensor"),
        P("tensor"),
        P("tensor", None),
        P(),
        P(),
        P(),
        P("dp", "tensor"),
        P(),
    )
    n_dp = mesh.shape["dp"]
    n_tensor = mesh.shape["tensor"]

    def run(*args):
        return body(*args, n_dp=n_dp, n_tensor=n_tensor)

    return jax.shard_map(
        run, mesh=mesh, in_specs=placed, out_specs=(P("dp", None), P("dp", None)), check_vma=False
    )
```

```python
import math

import jax
import jax.numpy as jnp
from jax import lax
from jax.sharding import PartitionSpec as P

HEAD = 64


def layer_norm(values, gain, shift):
    centre = jnp.mean(values, axis=-1, keepdims=True)
    centred = values - centre
    spread = jnp.mean(centred * centred, axis=-1, keepdims=True)
    return centred * lax.rsqrt(spread + 1e-05) * gain + shift


def segment_of(pack_lengths, count):
    ends = jnp.cumsum(pack_lengths)
    position = jnp.arange(count, dtype=jnp.int32)
    return jnp.sum((position[:, None] >= ends[None, :]).astype(jnp.int32), axis=1)


def is_power_of_two(n):
    return n >= 1 and (n & (n - 1)) == 0


def xor_pairs(n, k):
    return [(i, i ^ k) for i in range(n)]


def levels_of(n):
    return [1 << j for j in range(int(math.log2(n)))] if n > 1 else []


def reduce_scatter_xor(value, axis, n, levels):
    index = lax.axis_index(axis)
    acc = value
    block = 0
    count = 1
    for k in levels:
        half = acc.shape[0] // 2
        bit = (index // k) % 2
        mine = lax.dynamic_slice_in_dim(acc, bit * half, half, 0)
        theirs = lax.dynamic_slice_in_dim(acc, (1 - bit) * half, half, 0)
        wire = jnp.float32 if value.dtype == jnp.float32 else jnp.bfloat16
        got = lax.ppermute(theirs.astype(wire), axis, xor_pairs(n, k))
        acc = mine.astype(jnp.float32) + got.astype(jnp.float32)
        count *= 2
        block = block * 2 + bit
    return acc, block


def all_gather_xor(value, axis, n, levels):
    index = lax.axis_index(axis)
    cur = value
    for k in levels:
        other = lax.ppermute(cur, axis, xor_pairs(n, k))
        bit = (index // k) % 2
        cur = jnp.where(bit == 0, jnp.concatenate([cur, other]), jnp.concatenate([other, cur]))
    return cur


def settle(partial_value, residual, bias, gain, shift, n_tensor):
    if n_tensor == 4 and partial_value.shape[0] % 2 == 0:
        return settle_by_chip(partial_value, residual, bias, gain, shift)
    if not is_power_of_two(n_tensor) or partial_value.shape[0] % n_tensor:
        total = lax.psum(partial_value.astype(jnp.bfloat16), "tensor").astype(jnp.float32)
        return layer_norm(total + bias + residual.astype(jnp.float32), gain, shift).astype(
            jnp.bfloat16
        )
    levels = levels_of(n_tensor)
    total, block = reduce_scatter_xor(partial_value.astype(jnp.bfloat16), "tensor", n_tensor, levels)
    rows = total.shape[0]
    own_residual = lax.dynamic_slice_in_dim(residual, block * rows, rows, 0)
    normed = layer_norm(total + bias + own_residual.astype(jnp.float32), gain, shift).astype(
        jnp.bfloat16
    )
    return all_gather_xor(normed, "tensor", n_tensor, levels[::-1])


def settle_by_chip(partial_value, residual, bias, gain, shift):
    index = lax.axis_index("tensor")
    low = index % 2
    half = partial_value.shape[0] // 2
    rounded = partial_value.astype(jnp.bfloat16)
    mine = lax.dynamic_slice_in_dim(rounded, low * half, half, 0)
    theirs = lax.dynamic_slice_in_dim(rounded, (1 - low) * half, half, 0)
    got = lax.ppermute(theirs, "tensor", xor_pairs(4, 1))
    chip_sum = (mine.astype(jnp.float32) + got.astype(jnp.float32)).astype(jnp.bfloat16)
    across = lax.ppermute(chip_sum, "tensor", xor_pairs(4, 2))
    total = chip_sum.astype(jnp.float32) + across.astype(jnp.float32)
    own_residual = lax.dynamic_slice_in_dim(residual, low * half, half, 0)
    normed = layer_norm(total + bias + own_residual.astype(jnp.float32), gain, shift).astype(
        jnp.bfloat16
    )
    other = lax.ppermute(normed, "tensor", xor_pairs(4, 1))
    return jnp.where(low == 0, jnp.concatenate([normed, other]), jnp.concatenate([other, normed]))


def body(
    hidden,
    lengths,
    w_qkv,
    b_qkv,
    w_output,
    b_output,
    first_gain,
    first_shift,
    w_up,
    b_up,
    w_down,
    b_down,
    second_gain,
    second_shift,
    index,
    candidates,
    n_dp,
    n_tensor,
):
    tokens_here = hidden.shape[0]
    local_width = w_qkv.shape[2]
    local_heads = local_width // HEAD
    scale = jnp.array([0.125, 1.0, 1.0], jnp.float32)[:, None, None, None]
    projected = (
        (
            jnp.einsum(
                "td,jdhe->jhte",
                hidden,
                w_qkv.reshape(3, w_qkv.shape[1], local_heads, HEAD),
                preferred_element_type=jnp.float32,
            )
            + b_qkv.reshape(3, local_heads, 1, HEAD)
        )
        * scale
    ).astype(jnp.bfloat16)
    queries, keys, values = projected[0], projected[1], projected[2]
    segment = segment_of(lengths[0], tokens_here)
    same = segment[:, None] == segment[None, :]
    logits = jnp.einsum("htd,hsd->hts", queries, keys, preferred_element_type=jnp.float32)
    logits = jnp.where(same[None], logits, -1e30)
    top = jnp.max(logits, axis=-1, keepdims=True)
    expo = jnp.exp(logits - top)
    weights = (expo / jnp.sum(expo, axis=-1, keepdims=True)).astype(jnp.bfloat16)
    context = jnp.einsum("hts,hsd->thd", weights, values, preferred_element_type=jnp.float32)
    context = context.astype(jnp.bfloat16).reshape(tokens_here, local_width)
    partial_value = jnp.dot(context, w_output, preferred_element_type=jnp.float32)
    attended = settle(partial_value, hidden, b_output, first_gain, first_shift, n_tensor)
    activated = jax.nn.gelu(
        jnp.dot(attended, w_up, preferred_element_type=jnp.float32) + b_up, approximate=False
    ).astype(jnp.bfloat16)
    partial_value = jnp.dot(activated, w_down, preferred_element_type=jnp.float32)
    states = settle(partial_value, attended, b_down, second_gain, second_shift, n_tensor)
    texts_here = lengths.shape[1]
    member = (segment[None, :] == jnp.arange(texts_here, dtype=jnp.int32)[:, None]).astype(
        jnp.bfloat16
    )
    pooled = (
        jnp.dot(member, states, preferred_element_type=jnp.float32)
        / lengths[0].astype(jnp.float32)[:, None]
    )
    unit = pooled * lax.rsqrt(jnp.sum(pooled * pooled, axis=-1, keepdims=True) + 1e-06)
    quarter = index.shape[1]
    unit_quarter = lax.dynamic_slice_in_dim(
        unit, lax.axis_index("tensor") * quarter, quarter, 1
    ).astype(jnp.bfloat16)
    row_base = lax.axis_index("dp") * index.shape[0]
    xor_ok = (
        is_power_of_two(n_dp)
        and is_power_of_two(n_tensor)
        and candidates.shape[0] % n_dp == 0
    )
    if xor_ok:
        gathered = all_gather_xor(unit_quarter, "dp", n_dp, levels_of(n_dp))
    else:
        gathered = lax.all_gather(unit_quarter, "dp", axis=0, tiled=True)
    all_texts = candidates.shape[0]
    shard_rows = index.shape[0]
    local_rows = candidates - row_base
    held = (local_rows >= 0) & (local_rows < shard_rows)

    def pick(packed):
        units_block, wanted = packed
        texts = units_block.shape[0]
        tile = lax.dot_general(
            units_block, index, (((1,), (1,)), ((), ())), preferred_element_type=jnp.float32
        )
        minor = 128
        if shard_rows % minor == 0:
            major = shard_rows // minor
            major_hot = (
                (wanted // minor)[:, :, None] == jnp.arange(major, dtype=jnp.int32)[None, None, :]
            ).astype(jnp.bfloat16)
            high = tile.astype(jnp.bfloat16)
            low = (tile - high.astype(jnp.float32)).astype(jnp.bfloat16)
            parts = jnp.concatenate(
                [high.reshape(texts, major, minor), low.reshape(texts, major, minor)], axis=2
            )
            chosen_parts = jnp.einsum(
                "tca,tab->tcb", major_hot, parts, preferred_element_type=jnp.float32
            )
            rows_of = chosen_parts[:, :, :minor] + chosen_parts[:, :, minor:]
            minor_hot = (wanted % minor)[:, :, None] == jnp.arange(minor, dtype=jnp.int32)[None, None, :]
            picked = jnp.sum(jnp.where(minor_hot, rows_of, 0.0), axis=2)
        else:
            row_ids = jnp.arange(shard_rows, dtype=jnp.int32)
            chosen = wanted[:, :, None] == row_ids[None, None, :]
            picked = jnp.sum(jnp.where(chosen, tile[:, None, :], 0.0), axis=2)
        return picked

    wanted_all = jnp.clip(local_rows, 0, shard_rows - 1)
    block_rows = math.gcd(all_texts, 128)
    if block_rows == all_texts:
        picked = pick((gathered, wanted_all))
    else:
        picked = lax.map(
            pick,
            (
                gathered.reshape(all_texts // block_rows, block_rows, -1),
                wanted_all.reshape(all_texts // block_rows, block_rows, -1),
            ),
        ).reshape(all_texts, -1)
    partial_scores = jnp.where(held, picked, 0.0)
    if not xor_ok:
        slice_scores = lax.psum_scatter(
            partial_scores, ("dp", "tensor"), scatter_dimension=0, tiled=True
        )
        scores = lax.all_gather(slice_scores, "tensor", axis=0, tiled=True)
        return (states, scores)
    text_scores, _ = reduce_scatter_xor(partial_scores, "dp", n_dp, levels_of(n_dp)[::-1])
    for k in levels_of(n_tensor):
        text_scores = text_scores + lax.ppermute(text_scores, "tensor", xor_pairs(n_tensor, k))
    return (states, text_scores)


def solution(mesh):
    placed = (
        P("dp", None),
        P("dp", None),
        P(None, None, "tensor"),
        P(None, "tensor"),
        P("tensor", None),
        P(),
        P(),
        P(),
        P(None, "tensor"),
        P("tensor"),
        P("tensor", None),
        P(),
        P(),
        P(),
        P("dp", "tensor"),
        P(),
    )
    n_dp = mesh.shape["dp"]
    n_tensor = mesh.shape["tensor"]

    def run(*args):
        return body(*args, n_dp=n_dp, n_tensor=n_tensor)

    return jax.shard_map(
        run, mesh=mesh, in_specs=placed, out_specs=(P("dp", None), P("dp", None)), check_vma=False
    )
```

```python
import math

import jax
import jax.numpy as jnp
from jax import lax
from jax.sharding import PartitionSpec as P

HEAD = 64


def layer_norm(values, gain, shift):
    centre = jnp.mean(values, axis=-1, keepdims=True)
    centred = values - centre
    spread = jnp.mean(centred * centred, axis=-1, keepdims=True)
    return centred * lax.rsqrt(spread + 1e-05) * gain + shift


def segment_of(pack_lengths, count):
    ends = jnp.cumsum(pack_lengths)
    position = jnp.arange(count, dtype=jnp.int32)
    return jnp.sum((position[:, None] >= ends[None, :]).astype(jnp.int32), axis=1)


def is_power_of_two(n):
    return n >= 1 and (n & (n - 1)) == 0


def xor_pairs(n, k):
    return [(i, i ^ k) for i in range(n)]


def levels_of(n):
    return [1 << j for j in range(int(math.log2(n)))] if n > 1 else []


def reduce_scatter_xor(value, axis, n, levels):
    index = lax.axis_index(axis)
    acc = value
    block = 0
    count = 1
    for k in levels:
        half = acc.shape[0] // 2
        bit = (index // k) % 2
        mine = lax.dynamic_slice_in_dim(acc, bit * half, half, 0)
        theirs = lax.dynamic_slice_in_dim(acc, (1 - bit) * half, half, 0)
        wire = jnp.float32 if value.dtype == jnp.float32 else jnp.bfloat16
        got = lax.ppermute(theirs.astype(wire), axis, xor_pairs(n, k))
        acc = mine.astype(jnp.float32) + got.astype(jnp.float32)
        count *= 2
        block = block * 2 + bit
    return acc, block


def all_gather_xor(value, axis, n, levels):
    index = lax.axis_index(axis)
    cur = value
    for k in levels:
        other = lax.ppermute(cur, axis, xor_pairs(n, k))
        bit = (index // k) % 2
        cur = jnp.where(bit == 0, jnp.concatenate([cur, other]), jnp.concatenate([other, cur]))
    return cur


def settle(partial_value, residual, bias, gain, shift, n_tensor):
    if n_tensor == 4 and partial_value.shape[0] % 2 == 0:
        return settle_by_chip(partial_value, residual, bias, gain, shift)
    if not is_power_of_two(n_tensor) or partial_value.shape[0] % n_tensor:
        total = lax.psum(partial_value.astype(jnp.bfloat16), "tensor").astype(jnp.float32)
        return layer_norm(total + bias + residual.astype(jnp.float32), gain, shift).astype(
            jnp.bfloat16
        )
    levels = levels_of(n_tensor)
    total, block = reduce_scatter_xor(partial_value.astype(jnp.bfloat16), "tensor", n_tensor, levels)
    rows = total.shape[0]
    own_residual = lax.dynamic_slice_in_dim(residual, block * rows, rows, 0)
    normed = layer_norm(total + bias + own_residual.astype(jnp.float32), gain, shift).astype(
        jnp.bfloat16
    )
    return all_gather_xor(normed, "tensor", n_tensor, levels[::-1])


def settle_by_chip(partial_value, residual, bias, gain, shift):
    index = lax.axis_index("tensor")
    low = index % 2
    half = partial_value.shape[0] // 2
    rounded = partial_value.astype(jnp.bfloat16)
    mine = lax.dynamic_slice_in_dim(rounded, low * half, half, 0)
    theirs = lax.dynamic_slice_in_dim(rounded, (1 - low) * half, half, 0)
    got = lax.ppermute(theirs, "tensor", xor_pairs(4, 1))
    chip_sum = (mine.astype(jnp.float32) + got.astype(jnp.float32)).astype(jnp.bfloat16)
    across = lax.ppermute(chip_sum, "tensor", xor_pairs(4, 2))
    total = chip_sum.astype(jnp.float32) + across.astype(jnp.float32)
    own_residual = lax.dynamic_slice_in_dim(residual, low * half, half, 0)
    normed = layer_norm(total + bias + own_residual.astype(jnp.float32), gain, shift).astype(
        jnp.bfloat16
    )
    other = lax.ppermute(normed, "tensor", xor_pairs(4, 1))
    return jnp.where(low == 0, jnp.concatenate([normed, other]), jnp.concatenate([other, normed]))


def body(
    hidden,
    lengths,
    w_qkv,
    b_qkv,
    w_output,
    b_output,
    first_gain,
    first_shift,
    w_up,
    b_up,
    w_down,
    b_down,
    second_gain,
    second_shift,
    index,
    candidates,
    n_dp,
    n_tensor,
):
    tokens_here = hidden.shape[0]
    local_width = w_qkv.shape[2]
    local_heads = local_width // HEAD
    projected = (
        jnp.einsum("td,jdf->jtf", hidden, w_qkv, preferred_element_type=jnp.float32)
        + b_qkv[:, None, :]
    )
    queries = (projected[0] * 0.125).astype(jnp.bfloat16).reshape(tokens_here, local_heads, HEAD)
    keys = projected[1].astype(jnp.bfloat16).reshape(tokens_here, local_heads, HEAD)
    values = projected[2].astype(jnp.bfloat16).reshape(tokens_here, local_heads, HEAD)
    segment = segment_of(lengths[0], tokens_here)
    same = segment[:, None] == segment[None, :]
    logits = jnp.einsum("thd,shd->hts", queries, keys, preferred_element_type=jnp.float32)
    logits = jnp.where(same[None], logits, -1e30)
    top = jnp.max(logits, axis=-1, keepdims=True)
    expo = jnp.exp(logits - top)
    weights = (expo / jnp.sum(expo, axis=-1, keepdims=True)).astype(jnp.bfloat16)
    context = jnp.einsum("hts,shd->thd", weights, values, preferred_element_type=jnp.float32)
    context = context.astype(jnp.bfloat16).reshape(tokens_here, local_width)
    partial_value = jnp.dot(context, w_output, preferred_element_type=jnp.float32)
    attended = settle(partial_value, hidden, b_output, first_gain, first_shift, n_tensor)
    activated = jax.nn.gelu(
        jnp.dot(attended, w_up, preferred_element_type=jnp.float32) + b_up, approximate=False
    ).astype(jnp.bfloat16)
    partial_value = jnp.dot(activated, w_down, preferred_element_type=jnp.float32)
    states = settle(partial_value, attended, b_down, second_gain, second_shift, n_tensor)
    texts_here = lengths.shape[1]
    member = (segment[None, :] == jnp.arange(texts_here, dtype=jnp.int32)[:, None]).astype(
        jnp.bfloat16
    )
    pooled = (
        jnp.dot(member, states, preferred_element_type=jnp.float32)
        / lengths[0].astype(jnp.float32)[:, None]
    )
    unit = pooled * lax.rsqrt(jnp.sum(pooled * pooled, axis=-1, keepdims=True) + 1e-06)
    quarter = index.shape[1]
    unit_quarter = lax.dynamic_slice_in_dim(
        unit, lax.axis_index("tensor") * quarter, quarter, 1
    ).astype(jnp.bfloat16)
    row_base = lax.axis_index("dp") * index.shape[0]
    xor_ok = (
        is_power_of_two(n_dp)
        and is_power_of_two(n_tensor)
        and candidates.shape[0] % n_dp == 0
    )
    if xor_ok:
        dp_levels = levels_of(n_dp)
        gather_levels = dp_levels[-1:] + dp_levels[:-1]
        layout = gather_levels[::-1]
        gathered = all_gather_xor(unit_quarter, "dp", n_dp, gather_levels)
    else:
        gathered = lax.all_gather(unit_quarter, "dp", axis=0, tiled=True)
    all_texts = candidates.shape[0]
    shard_rows = index.shape[0]
    local_rows = candidates - row_base
    if xor_ok and n_dp > 1:
        bits = len(dp_levels)
        grouped = local_rows.reshape([2] * bits + [-1, local_rows.shape[1]])
        order = [bits - 1 - int(math.log2(k)) for k in layout]
        local_rows = grouped.transpose(order + [bits, bits + 1]).reshape(local_rows.shape)
    held = (local_rows >= 0) & (local_rows < shard_rows)

    def pick(packed):
        units_block, wanted = packed
        texts = units_block.shape[0]
        tile = lax.dot_general(
            units_block, index, (((1,), (1,)), ((), ())), preferred_element_type=jnp.float32
        )
        minor = 128
        if shard_rows % minor == 0:
            major = shard_rows // minor
            major_hot = (
                (wanted // minor)[:, :, None] == jnp.arange(major, dtype=jnp.int32)[None, None, :]
            ).astype(jnp.bfloat16)
            high = tile.astype(jnp.bfloat16)
            low = (tile - high.astype(jnp.float32)).astype(jnp.bfloat16)
            parts = jnp.concatenate(
                [high.reshape(texts, major, minor), low.reshape(texts, major, minor)], axis=2
            )
            chosen_parts = jnp.einsum(
                "tca,tab->tcb", major_hot, parts, preferred_element_type=jnp.float32
            )
            rows_of = chosen_parts[:, :, :minor] + chosen_parts[:, :, minor:]
            minor_hot = (wanted % minor)[:, :, None] == jnp.arange(minor, dtype=jnp.int32)[None, None, :]
            picked = jnp.sum(jnp.where(minor_hot, rows_of, 0.0), axis=2)
        else:
            row_ids = jnp.arange(shard_rows, dtype=jnp.int32)
            chosen = wanted[:, :, None] == row_ids[None, None, :]
            picked = jnp.sum(jnp.where(chosen, tile[:, None, :], 0.0), axis=2)
        return picked

    wanted_all = jnp.clip(local_rows, 0, shard_rows - 1)
    block_rows = math.gcd(all_texts, 128)
    if block_rows == all_texts:
        picked = pick((gathered, wanted_all))
    else:
        picked = lax.map(
            pick,
            (
                gathered.reshape(all_texts // block_rows, block_rows, -1),
                wanted_all.reshape(all_texts // block_rows, block_rows, -1),
            ),
        ).reshape(all_texts, -1)
    partial_scores = jnp.where(held, picked, 0.0)
    if not xor_ok:
        slice_scores = lax.psum_scatter(
            partial_scores, ("dp", "tensor"), scatter_dimension=0, tiled=True
        )
        scores = lax.all_gather(slice_scores, "tensor", axis=0, tiled=True)
        return (states, scores)
    text_scores, _ = reduce_scatter_xor(partial_scores, "dp", n_dp, layout)
    for k in levels_of(n_tensor):
        text_scores = text_scores + lax.ppermute(text_scores, "tensor", xor_pairs(n_tensor, k))
    return (states, text_scores)


def solution(mesh):
    placed = (
        P("dp", None),
        P("dp", None),
        P(None, None, "tensor"),
        P(None, "tensor"),
        P("tensor", None),
        P(),
        P(),
        P(),
        P(None, "tensor"),
        P("tensor"),
        P("tensor", None),
        P(),
        P(),
        P(),
        P("dp", "tensor"),
        P(),
    )
    n_dp = mesh.shape["dp"]
    n_tensor = mesh.shape["tensor"]

    def run(*args):
        return body(*args, n_dp=n_dp, n_tensor=n_tensor)

    return jax.shard_map(
        run, mesh=mesh, in_specs=placed, out_specs=(P("dp", None), P("dp", None)), check_vma=False
    )
```

```python
import math

import jax
import jax.numpy as jnp
from jax import lax
from jax.sharding import PartitionSpec as P

HEAD = 64


def layer_norm(values, gain, shift):
    centre = jnp.mean(values, axis=-1, keepdims=True)
    centred = values - centre
    spread = jnp.mean(centred * centred, axis=-1, keepdims=True)
    return centred * lax.rsqrt(spread + 1e-05) * gain + shift


def segment_of(pack_lengths, count):
    ends = jnp.cumsum(pack_lengths)
    position = jnp.arange(count, dtype=jnp.int32)
    return jnp.sum((position[:, None] >= ends[None, :]).astype(jnp.int32), axis=1)


def is_power_of_two(n):
    return n >= 1 and (n & (n - 1)) == 0


def xor_pairs(n, k):
    return [(i, i ^ k) for i in range(n)]


def levels_of(n):
    return [1 << j for j in range(int(math.log2(n)))] if n > 1 else []


def reduce_scatter_xor(value, axis, n, levels):
    index = lax.axis_index(axis)
    acc = value
    block = 0
    count = 1
    for k in levels:
        half = acc.shape[0] // 2
        bit = (index // k) % 2
        mine = lax.dynamic_slice_in_dim(acc, bit * half, half, 0)
        theirs = lax.dynamic_slice_in_dim(acc, (1 - bit) * half, half, 0)
        wire = jnp.float32 if value.dtype == jnp.float32 else jnp.bfloat16
        got = lax.ppermute(theirs.astype(wire), axis, xor_pairs(n, k))
        acc = mine.astype(jnp.float32) + got.astype(jnp.float32)
        count *= 2
        block = block * 2 + bit
    return acc, block


def all_gather_xor(value, axis, n, levels):
    index = lax.axis_index(axis)
    cur = value
    for k in levels:
        other = lax.ppermute(cur, axis, xor_pairs(n, k))
        bit = (index // k) % 2
        cur = jnp.where(bit == 0, jnp.concatenate([cur, other]), jnp.concatenate([other, cur]))
    return cur


def settle(partial_value, residual, bias, gain, shift, n_tensor):
    if n_tensor == 4 and partial_value.shape[0] % 2 == 0:
        return settle_by_chip(partial_value, residual, bias, gain, shift)
    if not is_power_of_two(n_tensor) or partial_value.shape[0] % n_tensor:
        total = lax.psum(partial_value.astype(jnp.bfloat16), "tensor").astype(jnp.float32)
        return layer_norm(total + bias + residual.astype(jnp.float32), gain, shift).astype(
            jnp.bfloat16
        )
    levels = levels_of(n_tensor)
    total, block = reduce_scatter_xor(partial_value.astype(jnp.bfloat16), "tensor", n_tensor, levels)
    rows = total.shape[0]
    own_residual = lax.dynamic_slice_in_dim(residual, block * rows, rows, 0)
    normed = layer_norm(total + bias + own_residual.astype(jnp.float32), gain, shift).astype(
        jnp.bfloat16
    )
    return all_gather_xor(normed, "tensor", n_tensor, levels[::-1])


def settle_by_chip(partial_value, residual, bias, gain, shift):
    index = lax.axis_index("tensor")
    low = index % 2
    half = partial_value.shape[0] // 2
    rounded = partial_value.astype(jnp.bfloat16)
    mine = lax.dynamic_slice_in_dim(rounded, low * half, half, 0)
    theirs = lax.dynamic_slice_in_dim(rounded, (1 - low) * half, half, 0)
    got = lax.ppermute(theirs, "tensor", xor_pairs(4, 1))
    chip_sum = (mine.astype(jnp.float32) + got.astype(jnp.float32)).astype(jnp.bfloat16)
    across = lax.ppermute(chip_sum, "tensor", xor_pairs(4, 2))
    total = chip_sum.astype(jnp.float32) + across.astype(jnp.float32)
    own_residual = lax.dynamic_slice_in_dim(residual, low * half, half, 0)
    normed = layer_norm(total + bias + own_residual.astype(jnp.float32), gain, shift).astype(
        jnp.bfloat16
    )
    other = lax.ppermute(normed, "tensor", xor_pairs(4, 1))
    return jnp.where(low == 0, jnp.concatenate([normed, other]), jnp.concatenate([other, normed]))


def body(
    hidden,
    lengths,
    w_qkv,
    b_qkv,
    w_output,
    b_output,
    first_gain,
    first_shift,
    w_up,
    b_up,
    w_down,
    b_down,
    second_gain,
    second_shift,
    index,
    candidates,
    n_dp,
    n_tensor,
):
    tokens_here = hidden.shape[0]
    local_width = w_qkv.shape[2]
    local_heads = local_width // HEAD
    projected = (
        jnp.einsum("td,jdf->jtf", hidden, w_qkv, preferred_element_type=jnp.float32)
        + b_qkv[:, None, :]
    )
    queries = (projected[0] * 0.125).astype(jnp.bfloat16).reshape(tokens_here, local_heads, HEAD)
    keys = projected[1].astype(jnp.bfloat16).reshape(tokens_here, local_heads, HEAD)
    values = projected[2].astype(jnp.bfloat16).reshape(tokens_here, local_heads, HEAD)
    segment = segment_of(lengths[0], tokens_here)
    same = segment[:, None] == segment[None, :]
    logits = jnp.einsum("thd,shd->hts", queries, keys, preferred_element_type=jnp.float32)
    logits = jnp.where(same[None], logits, -1e30)
    top = jnp.max(logits, axis=-1, keepdims=True)
    expo = jnp.exp(logits - top)
    weights = (expo / jnp.sum(expo, axis=-1, keepdims=True)).astype(jnp.bfloat16)
    context = jnp.einsum("hts,shd->thd", weights, values, preferred_element_type=jnp.float32)
    context = context.astype(jnp.bfloat16).reshape(tokens_here, local_width)
    partial_value = jnp.dot(context, w_output, preferred_element_type=jnp.float32)
    attended = settle(partial_value, hidden, b_output, first_gain, first_shift, n_tensor)
    activated = jax.nn.gelu(
        jnp.dot(attended, w_up, preferred_element_type=jnp.float32) + b_up, approximate=False
    ).astype(jnp.bfloat16)
    partial_value = jnp.dot(activated, w_down, preferred_element_type=jnp.float32)
    states = settle(partial_value, attended, b_down, second_gain, second_shift, n_tensor)
    texts_here = lengths.shape[1]
    member = (segment[None, :] == jnp.arange(texts_here, dtype=jnp.int32)[:, None]).astype(
        jnp.bfloat16
    )
    pooled = (
        jnp.dot(member, states, preferred_element_type=jnp.float32)
        / lengths[0].astype(jnp.float32)[:, None]
    )
    unit = pooled * lax.rsqrt(jnp.sum(pooled * pooled, axis=-1, keepdims=True) + 1e-06)
    quarter = index.shape[1]
    unit_quarter = lax.dynamic_slice_in_dim(
        unit, lax.axis_index("tensor") * quarter, quarter, 1
    ).astype(jnp.bfloat16)
    row_base = lax.axis_index("dp") * index.shape[0]
    xor_ok = (
        is_power_of_two(n_dp)
        and is_power_of_two(n_tensor)
        and candidates.shape[0] % n_dp == 0
    )
    if xor_ok:
        gathered = all_gather_xor(unit_quarter, "dp", n_dp, levels_of(n_dp))
    else:
        gathered = lax.all_gather(unit_quarter, "dp", axis=0, tiled=True)
    all_texts = candidates.shape[0]
    shard_rows = index.shape[0]
    local_rows = candidates - row_base
    held = (local_rows >= 0) & (local_rows < shard_rows)

    def pick(packed):
        units_block, wanted = packed
        texts = units_block.shape[0]
        tile = lax.dot_general(
            units_block, index, (((1,), (1,)), ((), ())), preferred_element_type=jnp.float32
        )
        minor = 128
        if shard_rows % minor == 0:
            major = shard_rows // minor
            minor_hot = (
                (wanted % minor)[:, :, None] == jnp.arange(minor, dtype=jnp.int32)[None, None, :]
            ).astype(jnp.bfloat16)
            high = tile.astype(jnp.bfloat16)
            low = (tile - high.astype(jnp.float32)).astype(jnp.bfloat16)
            parts = jnp.concatenate(
                [high.reshape(texts, major, minor), low.reshape(texts, major, minor)], axis=1
            )
            chosen_parts = jnp.einsum(
                "tcb,tab->tca", minor_hot, parts, preferred_element_type=jnp.float32
            )
            blocks_of = chosen_parts[:, :, :major] + chosen_parts[:, :, major:]
            major_hot = (wanted // minor)[:, :, None] == jnp.arange(major, dtype=jnp.int32)[None, None, :]
            picked = jnp.sum(jnp.where(major_hot, blocks_of, 0.0), axis=2)
        else:
            row_ids = jnp.arange(shard_rows, dtype=jnp.int32)
            chosen = wanted[:, :, None] == row_ids[None, None, :]
            picked = jnp.sum(jnp.where(chosen, tile[:, None, :], 0.0), axis=2)
        return picked

    wanted_all = jnp.clip(local_rows, 0, shard_rows - 1)
    block_rows = math.gcd(all_texts, 128)
    if block_rows == all_texts:
        picked = pick((gathered, wanted_all))
    else:
        picked = lax.map(
            pick,
            (
                gathered.reshape(all_texts // block_rows, block_rows, -1),
                wanted_all.reshape(all_texts // block_rows, block_rows, -1),
            ),
        ).reshape(all_texts, -1)
    partial_scores = jnp.where(held, picked, 0.0)
    if not xor_ok:
        slice_scores = lax.psum_scatter(
            partial_scores, ("dp", "tensor"), scatter_dimension=0, tiled=True
        )
        scores = lax.all_gather(slice_scores, "tensor", axis=0, tiled=True)
        return (states, scores)
    text_scores, _ = reduce_scatter_xor(partial_scores, "dp", n_dp, levels_of(n_dp)[::-1])
    for k in levels_of(n_tensor):
        text_scores = text_scores + lax.ppermute(text_scores, "tensor", xor_pairs(n_tensor, k))
    return (states, text_scores)


def solution(mesh):
    placed = (
        P("dp", None),
        P("dp", None),
        P(None, None, "tensor"),
        P(None, "tensor"),
        P("tensor", None),
        P(),
        P(),
        P(),
        P(None, "tensor"),
        P("tensor"),
        P("tensor", None),
        P(),
        P(),
        P(),
        P("dp", "tensor"),
        P(),
    )
    n_dp = mesh.shape["dp"]
    n_tensor = mesh.shape["tensor"]

    def run(*args):
        return body(*args, n_dp=n_dp, n_tensor=n_tensor)

    return jax.shard_map(
        run, mesh=mesh, in_specs=placed, out_specs=(P("dp", None), P("dp", None)), check_vma=False
    )
```

```python
import math

import jax
import jax.numpy as jnp
from jax import lax
from jax.sharding import PartitionSpec as P

HEAD = 64


def layer_norm(values, gain, shift):
    centre = jnp.mean(values, axis=-1, keepdims=True)
    centred = values - centre
    spread = jnp.mean(centred * centred, axis=-1, keepdims=True)
    return centred * lax.rsqrt(spread + 1e-05) * gain + shift


def segment_of(pack_lengths, count):
    ends = jnp.cumsum(pack_lengths)
    position = jnp.arange(count, dtype=jnp.int32)
    return jnp.sum((position[:, None] >= ends[None, :]).astype(jnp.int32), axis=1)


def is_power_of_two(n):
    return n >= 1 and (n & (n - 1)) == 0


def xor_pairs(n, k):
    return [(i, i ^ k) for i in range(n)]


def levels_of(n):
    return [1 << j for j in range(int(math.log2(n)))] if n > 1 else []


def reduce_scatter_xor(value, axis, n, levels):
    index = lax.axis_index(axis)
    acc = value
    block = 0
    count = 1
    for k in levels:
        half = acc.shape[0] // 2
        bit = (index // k) % 2
        mine = lax.dynamic_slice_in_dim(acc, bit * half, half, 0)
        theirs = lax.dynamic_slice_in_dim(acc, (1 - bit) * half, half, 0)
        wire = jnp.float32 if value.dtype == jnp.float32 else jnp.bfloat16
        got = lax.ppermute(theirs.astype(wire), axis, xor_pairs(n, k))
        acc = mine.astype(jnp.float32) + got.astype(jnp.float32)
        count *= 2
        block = block * 2 + bit
    return acc, block


def all_gather_xor(value, axis, n, levels):
    index = lax.axis_index(axis)
    cur = value
    for k in levels:
        other = lax.ppermute(cur, axis, xor_pairs(n, k))
        bit = (index // k) % 2
        cur = jnp.where(bit == 0, jnp.concatenate([cur, other]), jnp.concatenate([other, cur]))
    return cur


def settle(partial_value, residual, bias, gain, shift, n_tensor):
    if n_tensor == 4 and partial_value.shape[0] % 2 == 0:
        return settle_by_chip(partial_value, residual, bias, gain, shift)
    if not is_power_of_two(n_tensor) or partial_value.shape[0] % n_tensor:
        total = lax.psum(partial_value.astype(jnp.bfloat16), "tensor").astype(jnp.float32)
        return layer_norm(total + bias + residual.astype(jnp.float32), gain, shift).astype(
            jnp.bfloat16
        )
    levels = levels_of(n_tensor)
    total, block = reduce_scatter_xor(partial_value.astype(jnp.bfloat16), "tensor", n_tensor, levels)
    rows = total.shape[0]
    own_residual = lax.dynamic_slice_in_dim(residual, block * rows, rows, 0)
    normed = layer_norm(total + bias + own_residual.astype(jnp.float32), gain, shift).astype(
        jnp.bfloat16
    )
    return all_gather_xor(normed, "tensor", n_tensor, levels[::-1])


def settle_by_chip(partial_value, residual, bias, gain, shift):
    index = lax.axis_index("tensor")
    low = index % 2
    half = partial_value.shape[0] // 2
    rounded = partial_value.astype(jnp.bfloat16)
    mine = lax.dynamic_slice_in_dim(rounded, low * half, half, 0)
    theirs = lax.dynamic_slice_in_dim(rounded, (1 - low) * half, half, 0)
    got = lax.ppermute(theirs, "tensor", xor_pairs(4, 1))
    chip_sum = (mine.astype(jnp.float32) + got.astype(jnp.float32)).astype(jnp.bfloat16)
    across = lax.ppermute(chip_sum, "tensor", xor_pairs(4, 2))
    total = chip_sum.astype(jnp.float32) + across.astype(jnp.float32)
    own_residual = lax.dynamic_slice_in_dim(residual, low * half, half, 0)
    normed = layer_norm(total + bias + own_residual.astype(jnp.float32), gain, shift).astype(
        jnp.bfloat16
    )
    other = lax.ppermute(normed, "tensor", xor_pairs(4, 1))
    return jnp.where(low == 0, jnp.concatenate([normed, other]), jnp.concatenate([other, normed]))


def body(
    hidden,
    lengths,
    w_qkv,
    b_qkv,
    w_output,
    b_output,
    first_gain,
    first_shift,
    w_up,
    b_up,
    w_down,
    b_down,
    second_gain,
    second_shift,
    index,
    candidates,
    n_dp,
    n_tensor,
):
    tokens_here = hidden.shape[0]
    local_width = w_qkv.shape[2]
    local_heads = local_width // HEAD
    projected = (
        jnp.einsum("td,jdf->jtf", hidden, w_qkv, preferred_element_type=jnp.float32)
        + b_qkv[:, None, :]
    )
    queries = (projected[0] * 0.125).astype(jnp.bfloat16).reshape(tokens_here, local_heads, HEAD)
    keys = projected[1].astype(jnp.bfloat16).reshape(tokens_here, local_heads, HEAD)
    values = projected[2].astype(jnp.bfloat16).reshape(tokens_here, local_heads, HEAD)
    segment = segment_of(lengths[0], tokens_here)
    same = segment[:, None] == segment[None, :]
    logits = jnp.einsum("thd,shd->hts", queries, keys, preferred_element_type=jnp.float32)
    logits = jnp.where(same[None], logits, -1e30)
    top = jnp.max(logits, axis=-1, keepdims=True)
    expo = jnp.exp(logits - top)
    weights = (expo / jnp.sum(expo, axis=-1, keepdims=True)).astype(jnp.bfloat16)
    context = jnp.einsum("hts,shd->thd", weights, values, preferred_element_type=jnp.float32)
    context = context.astype(jnp.bfloat16).reshape(tokens_here, local_width)
    partial_value = jnp.dot(context, w_output, preferred_element_type=jnp.float32)
    attended = settle(partial_value, hidden, b_output, first_gain, first_shift, n_tensor)
    activated = jax.nn.gelu(
        jnp.dot(attended, w_up, preferred_element_type=jnp.float32) + b_up, approximate=False
    ).astype(jnp.bfloat16)
    partial_value = jnp.dot(activated, w_down, preferred_element_type=jnp.float32)
    states = settle(partial_value, attended, b_down, second_gain, second_shift, n_tensor)
    texts_here = lengths.shape[1]
    member = (segment[None, :] == jnp.arange(texts_here, dtype=jnp.int32)[:, None]).astype(
        jnp.bfloat16
    )
    pooled = (
        jnp.dot(member, states, preferred_element_type=jnp.float32)
        / lengths[0].astype(jnp.float32)[:, None]
    )
    unit = pooled * lax.rsqrt(jnp.sum(pooled * pooled, axis=-1, keepdims=True) + 1e-06)
    quarter = index.shape[1]
    unit_quarter = lax.dynamic_slice_in_dim(
        unit, lax.axis_index("tensor") * quarter, quarter, 1
    ).astype(jnp.bfloat16)
    row_base = lax.axis_index("dp") * index.shape[0]
    xor_ok = (
        is_power_of_two(n_dp)
        and is_power_of_two(n_tensor)
        and candidates.shape[0] % n_dp == 0
    )
    if xor_ok:
        gathered = all_gather_xor(unit_quarter, "dp", n_dp, levels_of(n_dp))
    else:
        gathered = lax.all_gather(unit_quarter, "dp", axis=0, tiled=True)
    all_texts = candidates.shape[0]
    shard_rows = index.shape[0]
    local_rows = candidates - row_base
    held = (local_rows >= 0) & (local_rows < shard_rows)

    def pick(packed):
        units_block, wanted = packed
        texts = units_block.shape[0]
        tile = lax.dot_general(
            units_block, index, (((1,), (1,)), ((), ())), preferred_element_type=jnp.float32
        )
        minor = 256
        if shard_rows % minor == 0:
            major = shard_rows // minor
            minor_hot = (
                (wanted % minor)[:, :, None] == jnp.arange(minor, dtype=jnp.int32)[None, None, :]
            ).astype(jnp.bfloat16)
            high = tile.astype(jnp.bfloat16)
            low = (tile - high.astype(jnp.float32)).astype(jnp.bfloat16)
            parts = jnp.concatenate(
                [high.reshape(texts, major, minor), low.reshape(texts, major, minor)], axis=1
            )
            chosen_parts = jnp.einsum(
                "tcb,tab->tca", minor_hot, parts, preferred_element_type=jnp.float32
            )
            blocks_of = chosen_parts[:, :, :major] + chosen_parts[:, :, major:]
            major_hot = (wanted // minor)[:, :, None] == jnp.arange(major, dtype=jnp.int32)[None, None, :]
            picked = jnp.sum(jnp.where(major_hot, blocks_of, 0.0), axis=2)
        else:
            row_ids = jnp.arange(shard_rows, dtype=jnp.int32)
            chosen = wanted[:, :, None] == row_ids[None, None, :]
            picked = jnp.sum(jnp.where(chosen, tile[:, None, :], 0.0), axis=2)
        return picked

    wanted_all = jnp.clip(local_rows, 0, shard_rows - 1)
    block_rows = math.gcd(all_texts, 128)
    if block_rows == all_texts:
        picked = pick((gathered, wanted_all))
    else:
        picked = lax.map(
            pick,
            (
                gathered.reshape(all_texts // block_rows, block_rows, -1),
                wanted_all.reshape(all_texts // block_rows, block_rows, -1),
            ),
        ).reshape(all_texts, -1)
    partial_scores = jnp.where(held, picked, 0.0)
    if not xor_ok:
        slice_scores = lax.psum_scatter(
            partial_scores, ("dp", "tensor"), scatter_dimension=0, tiled=True
        )
        scores = lax.all_gather(slice_scores, "tensor", axis=0, tiled=True)
        return (states, scores)
    text_scores, _ = reduce_scatter_xor(partial_scores, "dp", n_dp, levels_of(n_dp)[::-1])
    for k in levels_of(n_tensor):
        text_scores = text_scores + lax.ppermute(text_scores, "tensor", xor_pairs(n_tensor, k))
    return (states, text_scores)


def solution(mesh):
    placed = (
        P("dp", None),
        P("dp", None),
        P(None, None, "tensor"),
        P(None, "tensor"),
        P("tensor", None),
        P(),
        P(),
        P(),
        P(None, "tensor"),
        P("tensor"),
        P("tensor", None),
        P(),
        P(),
        P(),
        P("dp", "tensor"),
        P(),
    )
    n_dp = mesh.shape["dp"]
    n_tensor = mesh.shape["tensor"]

    def run(*args):
        return body(*args, n_dp=n_dp, n_tensor=n_tensor)

    return jax.shard_map(
        run, mesh=mesh, in_specs=placed, out_specs=(P("dp", None), P("dp", None)), check_vma=False
    )
```
